256 devices in a mesh: gz: 8 (over x, z_lo), gy: 32 (over z_hi, y, core).
Axes of the slice: x: 4, y: 4, z: 8 (z_hi: 4, z_lo: 2; z = z_hi * 2 + z_lo), core: 2. Of those that a mesh axis runs over, the one named last changes fastest.
Arguments:
- observed: float32 [256, 1024, 768], P('gz', 'gy'), may hold values from 0.2 to 5
- estimate: float32 [256, 1024, 768], P('gz', 'gy'), may hold values from 0.5 to 2
- taps_z: float32 [9], replicated, may hold values from 0.05 to 1
- taps_y: float32 [9], replicated, may hold values from 0.05 to 1
- taps_x: float32 [9], replicated, may hold values from 0.05 to 1
Outputs:
- updated: float32 [256, 1024, 768], P('gz', 'gy')
- projection: float32 [1024, 768], P('gy')
The draws below stay inside these ranges and needn't reach their ends.
All inputs are finite; a program needn't handle non-finite values.
Results may differ from the reference program's by a relative error of at most 0.00002.
Values sent between devices are 32-bit elements; how exact they have to be, the bound alone decides.
No kernel may reach another device: no remote copies, remote signals or barrier semaphores. Data moves between devices by JAX's collectives and lax.ppermute only.
A program may use at most 64 MiB of HBM per device.

```python
import math
import jax
import jax.numpy as jnp
from jax import lax

XCELLS = 768
TAPS = 9
YCELLS = 1024
ZCELLS = 256


def block_levels(key, extent, shards, least, top_value):
    gain = 1.0
    for position, parts in shards:
        heights = jax.random.uniform(jax.random.fold_in(jax.random.fold_in(key, 6), position), (parts,), jnp.float32, least / len(shards), top_value / len(shards))
        gain = gain * jnp.repeat(jnp.exp(heights), extent[position] // parts).reshape((-1,) + (1,) * (len(extent) - 1 - position))
    return gain


def setup_inputs(seed: int = 0) -> dict:
    streams_of = jax.random.split(jax.random.key(seed), 6)
    return {
        "observed": jnp.clip(jnp.exp(math.log(5.0) - 3.218876 * jax.random.uniform(streams_of[0], (ZCELLS, YCELLS, XCELLS), jnp.float32) ** block_levels(streams_of[0], (ZCELLS, YCELLS, XCELLS), ((0, 8), (1, 32)), -0.2, 0.2)), 0.2, 5.0),
        "estimate": jnp.clip(jnp.exp(math.log(2.0) - 1.3862944 * jax.random.uniform(streams_of[1], (ZCELLS, YCELLS, XCELLS), jnp.float32) ** block_levels(streams_of[1], (ZCELLS, YCELLS, XCELLS), ((0, 8), (1, 32)), -0.2, 0.2)), 0.5, 2.0),
        "taps_z": jnp.clip(jnp.exp(jax.random.uniform(streams_of[2], (TAPS,), jnp.float32, math.log(0.05), math.log(1.0))), 0.05, 1.0),
        "taps_y": jnp.clip(jnp.exp(jax.random.uniform(streams_of[3], (TAPS,), jnp.float32, math.log(0.05), math.log(1.0))), 0.05, 1.0),
        "taps_x": jnp.clip(jnp.exp(jax.random.uniform(streams_of[4], (TAPS,), jnp.float32, math.log(0.05), math.log(1.0))), 0.05, 1.0),
    }


def blur_axis(volume, taps, axis):
    radius = (taps.shape[0] - 1) // 2
    count = volume.shape[axis]
    widths = [(0, 0), (0, 0), (0, 0)]
    widths[axis] = (radius, radius)
    padded = jnp.pad(volume, widths)
    total = taps[0] * lax.slice_in_dim(padded, 0, count, axis=axis)
    for index in range(1, taps.shape[0]):
        total = total + taps[index] * lax.slice_in_dim(padded, index, index + count, axis=axis)
    return total


def blur_volume(volume, taps_z, taps_y, taps_x):
    volume = blur_axis(volume, taps_z, 0)
    volume = blur_axis(volume, taps_y, 1)
    return blur_axis(volume, taps_x, 2)


def reference(observed, estimate, taps_z, taps_y, taps_x):
    blurred = blur_volume(estimate, taps_z, taps_y, taps_x)
    ratio = observed / blurred
    correction = blur_volume(ratio, taps_z[::-1], taps_y[::-1], taps_x[::-1])
    updated = estimate * correction
    projection = jnp.max(updated, axis=0)
    return updated, projection
```

```python
import jax
import jax.numpy as jnp
from jax import lax
from jax.sharding import PartitionSpec as P


def with_halo(shard, sides, width):
    for axis, dim in sides:
        peers, length = (lax.axis_size(axis), shard.shape[dim])
        up = [(i, (i + 1) % peers) for i in range(peers - 1)]
        down = [(j, i) for i, j in up]
        last = lax.slice_in_dim(shard, length - width, length, axis=dim)
        first = lax.slice_in_dim(shard, 0, width, axis=dim)
        before = lax.ppermute(last, axis, up)
        after = lax.ppermute(first, axis, down)
        shard = jnp.concatenate([before, shard, after], axis=dim)
    return shard


def valid_pass(padded, taps, axis):
    count = padded.shape[axis] - (taps.shape[0] - 1)
    total = taps[0] * lax.slice_in_dim(padded, 0, count, axis=axis)
    for index in range(1, taps.shape[0]):
        total = total + taps[index] * lax.slice_in_dim(padded, index, index + count, axis=axis)
    return total


def blur_along_x(volume, taps):
    radius = (taps.shape[0] - 1) // 2
    padded = jnp.pad(volume, ((0, 0), (0, 0), (radius, radius)))
    return valid_pass(padded, taps, 2)


def blur_padded(padded, taps_z, taps_y, taps_x):
    volume = valid_pass(padded, taps_z, 0)
    volume = valid_pass(volume, taps_y, 1)
    return blur_along_x(volume, taps_x)


def butterfly_max(value, axis):
    peers = lax.axis_size(axis)
    step = 1
    while step < peers:
        pairs = [(i, i ^ step) for i in range(peers)]
        value = jnp.maximum(value, lax.ppermute(value, axis, pairs))
        step *= 2
    return value


def per_device(observed, estimate, taps_z, taps_y, taps_x):
    radius = (taps_z.shape[0] - 1) // 2
    back_z = taps_z[::-1]
    back_y = taps_y[::-1]
    back_x = taps_x[::-1]
    padded = with_halo(estimate, (("gz", 0), ("gy", 1)), radius)
    blurred = blur_padded(padded, taps_z, taps_y, taps_x)
    ratio = observed / blurred
    ratio_padded = with_halo(ratio, (("gz", 0), ("gy", 1)), radius)
    correction = blur_padded(ratio_padded, back_z, back_y, back_x)
    updated = estimate * correction
    local_max = jnp.max(updated, axis=0)
    projection = butterfly_max(local_max, "gz")
    return (updated, projection)


def solution(mesh):
    return jax.shard_map(
        per_device,
        mesh=mesh,
        in_specs=(P("gz", "gy", None), P("gz", "gy", None), P(), P(), P()),
        out_specs=(P("gz", "gy", None), P("gy", None)),
        check_vma=False,
    )
```

```python
import jax
import jax.numpy as jnp
from jax import lax
from jax.sharding import PartitionSpec as P


def shift_from(piece, axes, offsets):
    sizes = [lax.axis_size(a) for a in axes]
    pairs = []
    for src in range(sizes[0] * sizes[1]):
        coords = (src // sizes[1], src % sizes[1])
        dst = [c + o for c, o in zip(coords, offsets)]
        if all(0 <= d < n for d, n in zip(dst, sizes)):
            pairs.append((src, dst[0] * sizes[1] + dst[1]))
    return lax.ppermute(piece, axes, pairs)


def with_halo(shard, width):
    axes = ("gz", "gy")
    nz, ny = shard.shape[0], shard.shape[1]
    zs = {-1: slice(0, width), 0: slice(0, nz), 1: slice(nz - width, nz)}
    ys = {-1: slice(0, width), 0: slice(0, ny), 1: slice(ny - width, ny)}
    grid = {}
    for dz in (-1, 0, 1):
        for dy in (-1, 0, 1):
            if dz == 0 and dy == 0:
                grid[(dz, dy)] = shard
                continue
            piece = shard[zs[-dz], ys[-dy]]
            grid[(dz, dy)] = shift_from(piece, axes, (-dz, -dy))
    rows = [jnp.concatenate([grid[(dz, -1)], grid[(dz, 0)], grid[(dz, 1)]], axis=1) for dz in (-1, 0, 1)]
    return jnp.concatenate(rows, axis=0)


def valid_pass(padded, taps, axis):
    count = padded.shape[axis] - (taps.shape[0] - 1)
    total = taps[0] * lax.slice_in_dim(padded, 0, count, axis=axis)
    for index in range(1, taps.shape[0]):
        total = total + taps[index] * lax.slice_in_dim(padded, index, index + count, axis=axis)
    return total


def blur_along_x(volume, taps):
    radius = (taps.shape[0] - 1) // 2
    padded = jnp.pad(volume, ((0, 0), (0, 0), (radius, radius)))
    return valid_pass(padded, taps, 2)


def blur_padded(padded, taps_z, taps_y, taps_x):
    volume = valid_pass(padded, taps_z, 0)
    volume = valid_pass(volume, taps_y, 1)
    return blur_along_x(volume, taps_x)


def butterfly_max(value, axis):
    peers = lax.axis_size(axis)
    step = 1
    while step < peers:
        pairs = [(i, i ^ step) for i in range(peers)]
        value = jnp.maximum(value, lax.ppermute(value, axis, pairs))
        step *= 2
    return value


def per_device(observed, estimate, taps_z, taps_y, taps_x):
    radius = (taps_z.shape[0] - 1) // 2
    back_z = taps_z[::-1]
    back_y = taps_y[::-1]
    back_x = taps_x[::-1]
    padded = with_halo(estimate, radius)
    blurred = blur_padded(padded, taps_z, taps_y, taps_x)
    ratio = observed / blurred
    ratio_padded = with_halo(ratio, radius)
    correction = blur_padded(ratio_padded, back_z, back_y, back_x)
    updated = estimate * correction
    local_max = jnp.max(updated, axis=0)
    projection = butterfly_max(local_max, "gz")
    return (updated, projection)


def solution(mesh):
    return jax.shard_map(
        per_device,
        mesh=mesh,
        in_specs=(P("gz", "gy", None), P("gz", "gy", None), P(), P(), P()),
        out_specs=(P("gz", "gy", None), P("gy", None)),
        check_vma=False,
    )
```

```python
import jax
import jax.numpy as jnp
from jax import lax
from jax.sharding import PartitionSpec as P
import functools
from jax.experimental import pallas as pl
from jax.experimental.pallas import tpu as pltpu


def with_halo(shard, sides, width):
    for axis, dim in sides:
        peers, length = (lax.axis_size(axis), shard.shape[dim])
        up = [(i, (i + 1) % peers) for i in range(peers - 1)]
        down = [(j, i) for i, j in up]
        last = lax.slice_in_dim(shard, length - width, length, axis=dim)
        first = lax.slice_in_dim(shard, 0, width, axis=dim)
        before = lax.ppermute(last, axis, up)
        after = lax.ppermute(first, axis, down)
        shard = jnp.concatenate([before, shard, after], axis=dim)
    return shard


def valid_pass(padded, taps, axis):
    count = padded.shape[axis] - (taps.shape[0] - 1)
    total = taps[0] * lax.slice_in_dim(padded, 0, count, axis=axis)
    for index in range(1, taps.shape[0]):
        total = total + taps[index] * lax.slice_in_dim(padded, index, index + count, axis=axis)
    return total


def blur_along_x(volume, taps):
    radius = (taps.shape[0] - 1) // 2
    padded = jnp.pad(volume, ((0, 0), (0, 0), (radius, radius)))
    return valid_pass(padded, taps, 2)


def blur_padded(padded, taps_z, taps_y, taps_x):
    volume = valid_pass(padded, taps_z, 0)
    volume = valid_pass(volume, taps_y, 1)
    return blur_along_x(volume, taps_x)


def blur_kernel(mode, taps_ref, pad_ref, other_ref, out_ref, *rest):
    if mode == "update":
        max_ref, zbuf, ybuf = rest
    else:
        zbuf, ybuf = rest
    ntap = 9
    r = 4
    nz, ny, nx = out_ref.shape
    py = ny + 2 * r
    lanes = lax.broadcasted_iota(jnp.int32, (8, nx), 1)
    if mode == "update":
        max_ref[...] = jnp.full(max_ref.shape, -jnp.inf, max_ref.dtype)

    def plane(zo, carry):
        for c in range(py // 8):
            rows = pl.ds(c * 8, 8)
            acc = taps_ref[0] * pad_ref[zo, rows, :]
            for k in range(1, ntap):
                acc = acc + taps_ref[k] * pad_ref[zo + k, rows, :]
            zbuf[rows, :] = acc
        for c in range(ny // 8):
            acc = taps_ref[ntap] * zbuf[pl.ds(c * 8, 8), :]
            for k in range(1, ntap):
                acc = acc + taps_ref[ntap + k] * zbuf[pl.ds(c * 8 + k, 8), :]
            ybuf[pl.ds(c * 8, 8), :] = acc
        for c in range(ny // 8):
            rows = pl.ds(c * 8, 8)
            v = ybuf[rows, :]
            acc = None
            for k in range(ntap):
                d = k - r
                if d == 0:
                    s = v
                else:
                    s = pltpu.roll(v, (-d) % nx, 1)
                    keep = (lanes >= -d) if d < 0 else (lanes < nx - d)
                    s = jnp.where(keep, s, 0.0)
                term = taps_ref[2 * ntap + k] * s
                acc = term if acc is None else acc + term
            if mode == "ratio":
                out_ref[zo, rows, :] = other_ref[zo, rows, :] / acc
            else:
                upd = other_ref[zo, rows, :] * acc
                out_ref[zo, rows, :] = upd
                max_ref[rows, :] = jnp.maximum(max_ref[rows, :], upd)
        return carry

    lax.fori_loop(0, nz, plane, 0)


def fused_blur(mode, taps, padded, other):
    nz, ny, nx = other.shape
    vmem = pltpu.VMEM
    outs = [jax.ShapeDtypeStruct((nz, ny, nx), jnp.float32)]
    out_specs = [pl.BlockSpec(memory_space=vmem)]
    if mode == "update":
        outs.append(jax.ShapeDtypeStruct((ny, nx), jnp.float32))
        out_specs.append(pl.BlockSpec(memory_space=vmem))
    elems = nz * ny * nx
    return pl.pallas_call(
        functools.partial(blur_kernel, mode),
        out_shape=tuple(outs),
        in_specs=[pl.BlockSpec(memory_space=pltpu.SMEM), pl.BlockSpec(memory_space=vmem), pl.BlockSpec(memory_space=vmem)],
        out_specs=tuple(out_specs),
        scratch_shapes=[pltpu.VMEM((ny + 8, nx), jnp.float32), pltpu.VMEM((ny, nx), jnp.float32)],
        compiler_params=pltpu.CompilerParams(vmem_limit_bytes=48 * 1024 * 1024),
        cost_estimate=pl.CostEstimate(flops=elems * 60, bytes_accessed=elems * 4 * 4, transcendentals=0),
    )(taps, padded, other)


def butterfly_max(value, axis):
    peers = lax.axis_size(axis)
    step = 1
    while step < peers:
        pairs = [(i, i ^ step) for i in range(peers)]
        value = jnp.maximum(value, lax.ppermute(value, axis, pairs))
        step *= 2
    return value


def per_device(observed, estimate, taps_z, taps_y, taps_x):
    radius = (taps_z.shape[0] - 1) // 2
    forward = jnp.concatenate([taps_z, taps_y, taps_x])
    backward = jnp.concatenate([taps_z[::-1], taps_y[::-1], taps_x[::-1]])
    padded = with_halo(estimate, (("gz", 0), ("gy", 1)), radius)
    (ratio,) = fused_blur("ratio", forward, padded, observed)
    ratio_padded = with_halo(ratio, (("gz", 0), ("gy", 1)), radius)
    updated, local_max = fused_blur("update", backward, ratio_padded, estimate)
    projection = butterfly_max(local_max, "gz")
    return (updated, projection)


def solution(mesh):
    return jax.shard_map(
        per_device,
        mesh=mesh,
        in_specs=(P("gz", "gy", None), P("gz", "gy", None), P(), P(), P()),
        out_specs=(P("gz", "gy", None), P("gy", None)),
        check_vma=False,
    )
```

```python
import jax
import jax.numpy as jnp
from jax import lax
from jax.sharding import PartitionSpec as P
import functools
from jax.experimental import pallas as pl
from jax.experimental.pallas import tpu as pltpu


def blur_kernel(mode, segments, taps_ref, pad_ref, other_ref, out_ref, *rest):
    if mode == "update":
        max_ref, zbuf, ybuf = rest
    else:
        zbuf, ybuf = rest
    ntap = 9
    r = 4
    ny, nx = out_ref.shape[1], out_ref.shape[2]
    py = ny + 2 * r
    lanes = lax.broadcasted_iota(jnp.int32, (8, nx), 1)
    if mode == "update":
        max_ref[...] = jnp.full(max_ref.shape, -jnp.inf, max_ref.dtype)

    def plane(zo, zs, zt):
        for c in range(py // 8):
            rows = pl.ds(c * 8, 8)
            acc = taps_ref[0] * pad_ref[zs, rows, :]
            for k in range(1, ntap):
                acc = acc + taps_ref[k] * pad_ref[zs + k, rows, :]
            zbuf[rows, :] = acc
        for c in range(ny // 8):
            acc = taps_ref[ntap] * zbuf[pl.ds(c * 8, 8), :]
            for k in range(1, ntap):
                acc = acc + taps_ref[ntap + k] * zbuf[pl.ds(c * 8 + k, 8), :]
            ybuf[pl.ds(c * 8, 8), :] = acc
        for c in range(ny // 8):
            rows = pl.ds(c * 8, 8)
            v = ybuf[rows, :]
            acc = None
            for k in range(ntap):
                d = k - r
                if d == 0:
                    s = v
                else:
                    s = pltpu.roll(v, (-d) % nx, 1)
                    keep = (lanes >= -d) if d < 0 else (lanes < nx - d)
                    s = jnp.where(keep, s, 0.0)
                term = taps_ref[2 * ntap + k] * s
                acc = term if acc is None else acc + term
            if mode == "ratio":
                out_ref[zo, rows, :] = other_ref[zt, rows, :] / acc
            else:
                upd = other_ref[zt, rows, :] * acc
                out_ref[zo, rows, :] = upd
                max_ref[rows, :] = jnp.maximum(max_ref[rows, :], upd)

    for out_start, count, src_start, other_start in segments:
        def body(j, carry, out_start=out_start, src_start=src_start, other_start=other_start):
            plane(out_start + j, src_start + j, other_start + j)
            return carry

        lax.fori_loop(0, count, body, 0)


def fused_blur(mode, segments, taps, padded, other):
    nzo = sum(seg[1] for seg in segments)
    ny, nx = other.shape[1], other.shape[2]
    vmem = pltpu.VMEM
    outs = [jax.ShapeDtypeStruct((nzo, ny, nx), jnp.float32)]
    out_specs = [pl.BlockSpec(memory_space=vmem)]
    if mode == "update":
        outs.append(jax.ShapeDtypeStruct((ny, nx), jnp.float32))
        out_specs.append(pl.BlockSpec(memory_space=vmem))
    elems = nzo * ny * nx
    return pl.pallas_call(
        functools.partial(blur_kernel, mode, tuple(segments)),
        out_shape=tuple(outs),
        in_specs=[pl.BlockSpec(memory_space=pltpu.SMEM), pl.BlockSpec(memory_space=vmem), pl.BlockSpec(memory_space=vmem)],
        out_specs=tuple(out_specs),
        scratch_shapes=[pltpu.VMEM((ny + 8, nx), jnp.float32), pltpu.VMEM((ny, nx), jnp.float32)],
        compiler_params=pltpu.CompilerParams(vmem_limit_bytes=48 * 1024 * 1024),
        cost_estimate=pl.CostEstimate(flops=elems * 60, bytes_accessed=elems * 4 * 4, transcendentals=0),
    )(taps, padded, other)


def halo_pair(shard, axis, dim, width):
    peers, length = (lax.axis_size(axis), shard.shape[dim])
    up = [(i, (i + 1) % peers) for i in range(peers - 1)]
    down = [(j, i) for i, j in up]
    last = lax.slice_in_dim(shard, length - width, length, axis=dim)
    first = lax.slice_in_dim(shard, 0, width, axis=dim)
    before = lax.ppermute(last, axis, up)
    after = lax.ppermute(first, axis, down)
    return before, after


def split_blur(mode, taps, shard, other, width):
    nz = shard.shape[0]
    before, after = halo_pair(shard, "gy", 1, width)
    rows_padded = jnp.concatenate([before, shard, after], axis=1)
    below, above = halo_pair(rows_padded, "gz", 0, width)
    inner = fused_blur(mode, [(0, nz - 2 * width, 0, width)], taps, rows_padded, other)
    slabs = jnp.concatenate([below, rows_padded[: 2 * width], rows_padded[nz - 2 * width :], above], axis=0)
    edges = fused_blur(mode, [(0, width, 0, 0), (width, width, 3 * width, nz - width)], taps, slabs, other)
    volume = jnp.concatenate([edges[0][:width], inner[0], edges[0][width:]], axis=0)
    if mode == "update":
        return volume, jnp.maximum(inner[1], edges[1])
    return volume


def butterfly_max(value, axis):
    peers = lax.axis_size(axis)
    step = 1
    while step < peers:
        pairs = [(i, i ^ step) for i in range(peers)]
        value = jnp.maximum(value, lax.ppermute(value, axis, pairs))
        step *= 2
    return value


def per_device(observed, estimate, taps_z, taps_y, taps_x):
    radius = (taps_z.shape[0] - 1) // 2
    forward = jnp.concatenate([taps_z, taps_y, taps_x])
    backward = jnp.concatenate([taps_z[::-1], taps_y[::-1], taps_x[::-1]])
    ratio = split_blur("ratio", forward, estimate, observed, radius)
    updated, local_max = split_blur("update", backward, ratio, estimate, radius)
    projection = butterfly_max(local_max, "gz")
    return (updated, projection)


def solution(mesh):
    return jax.shard_map(
        per_device,
        mesh=mesh,
        in_specs=(P("gz", "gy", None), P("gz", "gy", None), P(), P(), P()),
        out_specs=(P("gz", "gy", None), P("gy", None)),
        check_vma=False,
    )
```

```python
import jax
import jax.numpy as jnp
from jax import lax
from jax.sharding import PartitionSpec as P
import functools

from jax.experimental import pallas as pl
from jax.experimental.pallas import tpu as pltpu


def blur_kernel(mode, segments, taps_ref, pad_ref, other_ref, out_ref, *rest):
    if mode == "update":
        max_ref, zbuf, ybuf = rest
    else:
        zbuf, ybuf = rest
    ntap = 9
    r = 4
    ny, nx = out_ref.shape[1], out_ref.shape[2]
    py = ny + 2 * r
    lanes = lax.broadcasted_iota(jnp.int32, (8, nx), 1)
    if mode == "update":
        max_ref[...] = jnp.full(max_ref.shape, -jnp.inf, max_ref.dtype)

    def plane(zo, zs, zt):
        for c in range(py // 8):
            rows = pl.ds(c * 8, 8)
            acc = taps_ref[0] * pad_ref[zs, rows, :]
            for k in range(1, ntap):
                acc = acc + taps_ref[k] * pad_ref[zs + k, rows, :]
            zbuf[rows, :] = acc
        for c in range(ny // 8):
            acc = taps_ref[ntap] * zbuf[pl.ds(c * 8, 8), :]
            for k in range(1, ntap):
                acc = acc + taps_ref[ntap + k] * zbuf[pl.ds(c * 8 + k, 8), :]
            ybuf[pl.ds(c * 8, 8), :] = acc
        for c in range(ny // 8):
            rows = pl.ds(c * 8, 8)
            v = ybuf[rows, :]
            acc = None
            for k in range(ntap):
                d = k - r
                if d == 0:
                    s = v
                else:
                    s = pltpu.roll(v, (-d) % nx, 1)
                    keep = (lanes >= -d) if d < 0 else (lanes < nx - d)
                    s = jnp.where(keep, s, 0.0)
                term = taps_ref[2 * ntap + k] * s
                acc = term if acc is None else acc + term
            if mode == "ratio":
                out_ref[zo, rows, :] = other_ref[zt, rows, :] / acc
            else:
                upd = other_ref[zt, rows, :] * acc
                out_ref[zo, rows, :] = upd
                max_ref[rows, :] = jnp.maximum(max_ref[rows, :], upd)

    for out_start, count, src_start, other_start in segments:
        def body(j, carry, out_start=out_start, src_start=src_start, other_start=other_start):
            plane(out_start + j, src_start + j, other_start + j)
            return carry

        lax.fori_loop(0, count, body, 0)


def fused_blur(mode, segments, taps, padded, other):
    nzo = sum(seg[1] for seg in segments)
    ny, nx = other.shape[1], other.shape[2]
    vmem = pltpu.VMEM
    outs = [jax.ShapeDtypeStruct((nzo, ny, nx), jnp.float32)]
    out_specs = [pl.BlockSpec(memory_space=vmem)]
    if mode == "update":
        outs.append(jax.ShapeDtypeStruct((ny, nx), jnp.float32))
        out_specs.append(pl.BlockSpec(memory_space=vmem))
    elems = nzo * ny * nx
    return pl.pallas_call(
        functools.partial(blur_kernel, mode, tuple(segments)),
        out_shape=tuple(outs),
        in_specs=[pl.BlockSpec(memory_space=pltpu.SMEM), pl.BlockSpec(memory_space=vmem), pl.BlockSpec(memory_space=vmem)],
        out_specs=tuple(out_specs),
        scratch_shapes=[pltpu.VMEM((ny + 8, nx), jnp.float32), pltpu.VMEM((ny, nx), jnp.float32)],
        compiler_params=pltpu.CompilerParams(vmem_limit_bytes=48 * 1024 * 1024),
        cost_estimate=pl.CostEstimate(flops=elems * 60, bytes_accessed=elems * 4 * 4, transcendentals=0),
    )(taps, padded, other)


def halo_pair(shard, axis, dim, width):
    peers, length = (lax.axis_size(axis), shard.shape[dim])
    up = [(i, (i + 1) % peers) for i in range(peers - 1)]
    down = [(j, i) for i, j in up]
    last = lax.slice_in_dim(shard, length - width, length, axis=dim)
    first = lax.slice_in_dim(shard, 0, width, axis=dim)
    before = lax.ppermute(last, axis, up)
    after = lax.ppermute(first, axis, down)
    return before, after


def split_blur(mode, taps, shard, other, width):
    nz = shard.shape[0]
    before, after = halo_pair(shard, "gy", 1, width)
    rows_padded = jnp.concatenate([before, shard, after], axis=1)
    below, above = halo_pair(rows_padded, "gz", 0, width)
    inner = fused_blur(mode, [(0, nz - 2 * width, 0, width)], taps, rows_padded, other)
    slabs = jnp.concatenate([below, rows_padded[: 2 * width], rows_padded[nz - 2 * width :], above], axis=0)
    edges = fused_blur(mode, [(0, width, 0, 0), (width, width, 3 * width, nz - width)], taps, slabs, other)
    volume = jnp.concatenate([edges[0][:width], inner[0], edges[0][width:]], axis=0)
    if mode == "update":
        return volume, jnp.maximum(inner[1], edges[1])
    return volume


def gathered_max(value, axis):
    peers = lax.axis_size(axis)
    result = value
    for shift in range(1, peers):
        pairs = [(i, (i + shift) % peers) for i in range(peers)]
        result = jnp.maximum(result, lax.ppermute(value, axis, pairs))
    return result


def per_device(observed, estimate, taps_z, taps_y, taps_x):
    radius = (taps_z.shape[0] - 1) // 2
    forward = jnp.concatenate([taps_z, taps_y, taps_x])
    backward = jnp.concatenate([taps_z[::-1], taps_y[::-1], taps_x[::-1]])
    ratio = split_blur("ratio", forward, estimate, observed, radius)
    updated, local_max = split_blur("update", backward, ratio, estimate, radius)
    projection = gathered_max(local_max, "gz")
    return (updated, projection)


def solution(mesh):
    return jax.shard_map(
        per_device,
        mesh=mesh,
        in_specs=(P("gz", "gy", None), P("gz", "gy", None), P(), P(), P()),
        out_specs=(P("gz", "gy", None), P("gy", None)),
        check_vma=False,
    )
```

```python
import jax
import jax.numpy as jnp
from jax import lax
from jax.sharding import PartitionSpec as P
import functools
from jax.experimental import pallas as pl
from jax.experimental.pallas import tpu as pltpu


def blur_kernel(mode, segments, taps_ref, pad_ref, other_ref, out_ref, *rest):
    if mode == "update":
        max_ref, zbuf, ybuf = rest
    else:
        zbuf, ybuf = rest
    ntap = 9
    r = 4
    ny, nx = out_ref.shape[1], out_ref.shape[2]
    py = ny + 2 * r
    lanes = lax.broadcasted_iota(jnp.int32, (8, nx), 1)
    if mode == "update":
        max_ref[...] = jnp.full(max_ref.shape, -jnp.inf, max_ref.dtype)

    def plane(zo, zs, zt):
        for c in range(py // 8):
            rows = pl.ds(c * 8, 8)
            acc = taps_ref[0] * pad_ref[zs, rows, :]
            for k in range(1, ntap):
                acc = acc + taps_ref[k] * pad_ref[zs + k, rows, :]
            zbuf[rows, :] = acc
        for c in range(ny // 8):
            acc = taps_ref[ntap] * zbuf[pl.ds(c * 8, 8), :]
            for k in range(1, ntap):
                acc = acc + taps_ref[ntap + k] * zbuf[pl.ds(c * 8 + k, 8), :]
            ybuf[pl.ds(c * 8, 8), :] = acc
        for c in range(ny // 8):
            rows = pl.ds(c * 8, 8)
            v = ybuf[rows, :]
            acc = None
            for k in range(ntap):
                d = k - r
                if d == 0:
                    s = v
                else:
                    s = pltpu.roll(v, (-d) % nx, 1)
                    keep = (lanes >= -d) if d < 0 else (lanes < nx - d)
                    s = jnp.where(keep, s, 0.0)
                term = taps_ref[2 * ntap + k] * s
                acc = term if acc is None else acc + term
            if mode == "ratio":
                out_ref[zo, rows, :] = other_ref[zt, rows, :] / acc
            else:
                upd = other_ref[zt, rows, :] * acc
                out_ref[zo, rows, :] = upd
                max_ref[rows, :] = jnp.maximum(max_ref[rows, :], upd)

    for out_start, count, src_start, other_start in segments:
        def body(j, carry, out_start=out_start, src_start=src_start, other_start=other_start):
            plane(out_start + j, src_start + j, other_start + j)
            return carry

        lax.fori_loop(0, count, body, 0)


def fused_blur(mode, segments, taps, padded, other):
    nzo = sum(seg[1] for seg in segments)
    ny, nx = other.shape[1], other.shape[2]
    vmem = pltpu.VMEM
    outs = [jax.ShapeDtypeStruct((nzo, ny, nx), jnp.float32)]
    out_specs = [pl.BlockSpec(memory_space=vmem)]
    if mode == "update":
        outs.append(jax.ShapeDtypeStruct((ny, nx), jnp.float32))
        out_specs.append(pl.BlockSpec(memory_space=vmem))
    elems = nzo * ny * nx
    return pl.pallas_call(
        functools.partial(blur_kernel, mode, tuple(segments)),
        out_shape=tuple(outs),
        in_specs=[pl.BlockSpec(memory_space=pltpu.SMEM), pl.BlockSpec(memory_space=vmem), pl.BlockSpec(memory_space=vmem)],
        out_specs=tuple(out_specs),
        scratch_shapes=[pltpu.VMEM((ny + 8, nx), jnp.float32), pltpu.VMEM((ny, nx), jnp.float32)],
        compiler_params=pltpu.CompilerParams(vmem_limit_bytes=48 * 1024 * 1024),
        cost_estimate=pl.CostEstimate(flops=elems * 60, bytes_accessed=elems * 4 * 4, transcendentals=0),
    )(taps, padded, other)


def halo_pair(shard, axis, dim, width):
    peers, length = (lax.axis_size(axis), shard.shape[dim])
    up = [(i, (i + 1) % peers) for i in range(peers - 1)]
    down = [(j, i) for i, j in up]
    last = lax.slice_in_dim(shard, length - width, length, axis=dim)
    first = lax.slice_in_dim(shard, 0, width, axis=dim)
    before = lax.ppermute(last, axis, up)
    after = lax.ppermute(first, axis, down)
    return before, after


def split_blur(mode, taps, shard, other, width):
    nz = shard.shape[0]
    before, after = halo_pair(shard, "gy", 1, width)
    below, above = halo_pair(shard, "gz", 0, width)
    side_rows = jnp.concatenate([before, after], axis=1)
    corner_below, corner_above = halo_pair(side_rows, "gz", 0, width)
    rows_padded = jnp.concatenate([before, shard, after], axis=1)
    inner = fused_blur(mode, [(0, nz - 2 * width, 0, width)], taps, rows_padded, other)
    below_padded = jnp.concatenate([corner_below[:, :width], below, corner_below[:, width:]], axis=1)
    above_padded = jnp.concatenate([corner_above[:, :width], above, corner_above[:, width:]], axis=1)
    slabs = jnp.concatenate([below_padded, rows_padded[: 2 * width], rows_padded[nz - 2 * width :], above_padded], axis=0)
    edges = fused_blur(mode, [(0, width, 0, 0), (width, width, 3 * width, nz - width)], taps, slabs, other)
    volume = jnp.concatenate([edges[0][:width], inner[0], edges[0][width:]], axis=0)
    if mode == "update":
        return volume, jnp.maximum(inner[1], edges[1])
    return volume


def butterfly_max(value, axis):
    peers = lax.axis_size(axis)
    step = 1
    while step < peers:
        pairs = [(i, i ^ step) for i in range(peers)]
        value = jnp.maximum(value, lax.ppermute(value, axis, pairs))
        step *= 2
    return value


def per_device(observed, estimate, taps_z, taps_y, taps_x):
    radius = (taps_z.shape[0] - 1) // 2
    forward = jnp.concatenate([taps_z, taps_y, taps_x])
    backward = jnp.concatenate([taps_z[::-1], taps_y[::-1], taps_x[::-1]])
    ratio = split_blur("ratio", forward, estimate, observed, radius)
    updated, local_max = split_blur("update", backward, ratio, estimate, radius)
    projection = butterfly_max(local_max, "gz")
    return (updated, projection)


def solution(mesh):
    return jax.shard_map(
        per_device,
        mesh=mesh,
        in_specs=(P("gz", "gy", None), P("gz", "gy", None), P(), P(), P()),
        out_specs=(P("gz", "gy", None), P("gy", None)),
        check_vma=False,
    )
```

```python
import jax
import jax.numpy as jnp
from jax import lax
from jax.sharding import PartitionSpec as P
import functools
from jax.experimental import pallas as pl
from jax.experimental.pallas import tpu as pltpu


def plane_blur(mode, taps_ref, load, zbuf, ybuf, lanes, store, other_plane, max_ref):
    ntap = 9
    r = 4
    ny, nx = ybuf.shape
    py = ny + 2 * r
    for c in range(py // 8):
        rows = pl.ds(c * 8, 8)
        acc = taps_ref[0] * load(0, rows)
        for k in range(1, ntap):
            acc = acc + taps_ref[k] * load(k, rows)
        zbuf[rows, :] = acc
    for c in range(ny // 8):
        acc = taps_ref[ntap] * zbuf[pl.ds(c * 8, 8), :]
        for k in range(1, ntap):
            acc = acc + taps_ref[ntap + k] * zbuf[pl.ds(c * 8 + k, 8), :]
        ybuf[pl.ds(c * 8, 8), :] = acc
    for c in range(ny // 8):
        rows = pl.ds(c * 8, 8)
        v = ybuf[rows, :]
        acc = None
        for k in range(ntap):
            d = k - r
            if d == 0:
                s = v
            else:
                s = pltpu.roll(v, (-d) % nx, 1)
                keep = (lanes >= -d) if d < 0 else (lanes < nx - d)
                s = jnp.where(keep, s, 0.0)
            term = taps_ref[2 * ntap + k] * s
            acc = term if acc is None else acc + term
        if mode == "ratio":
            store(rows, other_plane(rows) / acc)
        else:
            upd = other_plane(rows) * acc
            store(rows, upd)
            max_ref[rows, :] = jnp.maximum(max_ref[rows, :], upd)


def inner_kernel(mode, width, taps_ref, pad_ref, other_ref, out_ref, *rest):
    if mode == "update":
        max_ref, zbuf, ybuf = rest
        max_ref[...] = jnp.full(max_ref.shape, -jnp.inf, max_ref.dtype)
    else:
        (zbuf, ybuf), max_ref = rest, None
    nz, nx = out_ref.shape[0], out_ref.shape[2]
    lanes = lax.broadcasted_iota(jnp.int32, (8, nx), 1)

    def body(j, carry):
        zo = width + j

        def load(k, rows):
            return pad_ref[j + k, rows, :]

        def store(rows, value):
            out_ref[zo, rows, :] = value

        plane_blur(mode, taps_ref, load, zbuf, ybuf, lanes, store, lambda rows: other_ref[zo, rows, :], max_ref)
        return carry

    lax.fori_loop(0, nz - 2 * width, body, 0)


def edge_kernel(mode, width, taps_ref, below_ref, pad_ref, above_ref, other_ref, volume_in, volume_ref, *rest):
    if mode == "update":
        max_ref, planes, zbuf, ybuf, sems = rest
        max_ref[...] = jnp.full(max_ref.shape, -jnp.inf, max_ref.dtype)
    else:
        (planes, zbuf, ybuf, sems), max_ref = rest, None
    nz, nx = pad_ref.shape[0], pad_ref.shape[2]
    lanes = lax.broadcasted_iota(jnp.int32, (8, nx), 1)
    outs = list(range(width)) + list(range(nz - width, nz))
    for slot, zo in enumerate(outs):

        def load(k, rows, zo=zo):
            q = zo + k
            if q < width:
                return below_ref[q, rows, :]
            if q >= nz + width:
                return above_ref[q - nz - width, rows, :]
            return pad_ref[q - width, rows, :]

        def store(rows, value, slot=slot):
            planes[slot, rows, :] = value

        plane_blur(mode, taps_ref, load, zbuf, ybuf, lanes, store, lambda rows, zo=zo: other_ref[zo, rows, :], max_ref)
    low = pltpu.make_async_copy(planes.at[pl.ds(0, width)], volume_ref.at[pl.ds(0, width)], sems.at[0])
    high = pltpu.make_async_copy(planes.at[pl.ds(width, width)], volume_ref.at[pl.ds(nz - width, width)], sems.at[1])
    low.start()
    high.start()
    low.wait()
    high.wait()


def inner_blur(mode, width, taps, padded, other):
    nz, ny, nx = other.shape
    vmem = pltpu.VMEM
    outs = [jax.ShapeDtypeStruct((nz, ny, nx), jnp.float32)]
    out_specs = [pl.BlockSpec(memory_space=vmem)]
    if mode == "update":
        outs.append(jax.ShapeDtypeStruct((ny, nx), jnp.float32))
        out_specs.append(pl.BlockSpec(memory_space=vmem))
    elems = (nz - 2 * width) * ny * nx
    return pl.pallas_call(
        functools.partial(inner_kernel, mode, width),
        out_shape=tuple(outs),
        in_specs=[pl.BlockSpec(memory_space=pltpu.SMEM), pl.BlockSpec(memory_space=vmem), pl.BlockSpec(memory_space=vmem)],
        out_specs=tuple(out_specs),
        scratch_shapes=[pltpu.VMEM((ny + 8, nx), jnp.float32), pltpu.VMEM((ny, nx), jnp.float32)],
        compiler_params=pltpu.CompilerParams(vmem_limit_bytes=48 * 1024 * 1024),
        cost_estimate=pl.CostEstimate(flops=elems * 60, bytes_accessed=elems * 4 * 4, transcendentals=0),
    )(taps, padded, other)


def edge_blur(mode, width, taps, below, padded, above, other, volume):
    nz, ny, nx = other.shape
    vmem = pltpu.VMEM
    outs = [jax.ShapeDtypeStruct((nz, ny, nx), jnp.float32)]
    out_specs = [pl.BlockSpec(memory_space=pl.ANY)]
    if mode == "update":
        outs.append(jax.ShapeDtypeStruct((ny, nx), jnp.float32))
        out_specs.append(pl.BlockSpec(memory_space=vmem))
    elems = 2 * width * ny * nx
    return pl.pallas_call(
        functools.partial(edge_kernel, mode, width),
        out_shape=tuple(outs),
        in_specs=[pl.BlockSpec(memory_space=pltpu.SMEM)] + [pl.BlockSpec(memory_space=vmem)] * 4 + [pl.BlockSpec(memory_space=pl.ANY)],
        out_specs=tuple(out_specs),
        scratch_shapes=[
            pltpu.VMEM((2 * width, ny, nx), jnp.float32),
            pltpu.VMEM((ny + 8, nx), jnp.float32),
            pltpu.VMEM((ny, nx), jnp.float32),
            pltpu.SemaphoreType.DMA((2,)),
        ],
        input_output_aliases={5: 0},
        compiler_params=pltpu.CompilerParams(vmem_limit_bytes=48 * 1024 * 1024),
        cost_estimate=pl.CostEstimate(flops=elems * 60, bytes_accessed=elems * 4 * 4, transcendentals=0),
    )(taps, below, padded, above, other, volume)


def halo_pair(shard, axis, dim, width):
    peers, length = (lax.axis_size(axis), shard.shape[dim])
    up = [(i, (i + 1) % peers) for i in range(peers - 1)]
    down = [(j, i) for i, j in up]
    last = lax.slice_in_dim(shard, length - width, length, axis=dim)
    first = lax.slice_in_dim(shard, 0, width, axis=dim)
    before = lax.ppermute(last, axis, up)
    after = lax.ppermute(first, axis, down)
    return before, after


def split_blur(mode, taps, shard, other, width):
    before, after = halo_pair(shard, "gy", 1, width)
    rows_padded = jnp.concatenate([before, shard, after], axis=1)
    below, above = halo_pair(rows_padded, "gz", 0, width)
    inner = inner_blur(mode, width, taps, rows_padded, other)
    edges = edge_blur(mode, width, taps, below, rows_padded, above, other, inner[0])
    if mode == "update":
        return edges[0], jnp.maximum(inner[1], edges[1])
    return edges[0]


def butterfly_max(value, axis):
    peers = lax.axis_size(axis)
    step = 1
    while step < peers:
        pairs = [(i, i ^ step) for i in range(peers)]
        value = jnp.maximum(value, lax.ppermute(value, axis, pairs))
        step *= 2
    return value


def per_device(observed, estimate, taps_z, taps_y, taps_x):
    radius = (taps_z.shape[0] - 1) // 2
    forward = jnp.concatenate([taps_z, taps_y, taps_x])
    backward = jnp.concatenate([taps_z[::-1], taps_y[::-1], taps_x[::-1]])
    ratio = split_blur("ratio", forward, estimate, observed, radius)
    updated, local_max = split_blur("update", backward, ratio, estimate, radius)
    projection = butterfly_max(local_max, "gz")
    return (updated, projection)


def solution(mesh):
    return jax.shard_map(
        per_device,
        mesh=mesh,
        in_specs=(P("gz", "gy", None), P("gz", "gy", None), P(), P(), P()),
        out_specs=(P("gz", "gy", None), P("gy", None)),
        check_vma=False,
    )
```

```python
import jax
import jax.numpy as jnp
from jax import lax
from jax.sharding import PartitionSpec as P
import functools
from jax.experimental import pallas as pl
from jax.experimental.pallas import tpu as pltpu


def plane_blur(mode, taps_ref, load, zbuf, ybuf, lanes, store, other_plane, max_ref):
    ntap = 9
    r = 4
    ny, nx = ybuf.shape
    py = ny + 2 * r
    for c in range(py // 8):
        rows = pl.ds(c * 8, 8)
        acc = taps_ref[0] * load(0, rows)
        for k in range(1, ntap):
            acc = acc + taps_ref[k] * load(k, rows)
        zbuf[rows, :] = acc
    for c in range(ny // 8):
        acc = taps_ref[ntap] * zbuf[pl.ds(c * 8, 8), :]
        for k in range(1, ntap):
            acc = acc + taps_ref[ntap + k] * zbuf[pl.ds(c * 8 + k, 8), :]
        ybuf[pl.ds(c * 8, 8), :] = acc
    for c in range(ny // 8):
        rows = pl.ds(c * 8, 8)
        v = ybuf[rows, :]
        acc = None
        for k in range(ntap):
            d = k - r
            if d == 0:
                s = v
            else:
                s = pltpu.roll(v, (-d) % nx, 1)
                keep = (lanes >= -d) if d < 0 else (lanes < nx - d)
                s = jnp.where(keep, s, 0.0)
            term = taps_ref[2 * ntap + k] * s
            acc = term if acc is None else acc + term
        if mode == "ratio":
            store(rows, other_plane(rows) / acc)
        else:
            upd = other_plane(rows) * acc
            store(rows, upd)
            max_ref[rows, :] = jnp.maximum(max_ref[rows, :], upd)


def inner_kernel(mode, width, taps_ref, pad_ref, other_ref, out_ref, *rest):
    if mode == "update":
        max_ref, zbuf, ybuf = rest
        max_ref[...] = jnp.full(max_ref.shape, -jnp.inf, max_ref.dtype)
    else:
        (zbuf, ybuf), max_ref = rest, None
    nz, nx = out_ref.shape[0], out_ref.shape[2]
    lanes = lax.broadcasted_iota(jnp.int32, (8, nx), 1)

    def body(j, carry):
        zo = width + j

        def load(k, rows):
            return pad_ref[j + k, rows, :]

        def store(rows, value):
            out_ref[zo, rows, :] = value

        plane_blur(mode, taps_ref, load, zbuf, ybuf, lanes, store, lambda rows: other_ref[zo, rows, :], max_ref)
        return carry

    lax.fori_loop(0, nz - 2 * width, body, 0)


def edge_kernel(mode, width, taps_ref, below_ref, pad_ref, above_ref, other_ref, volume_in, volume_ref, *rest):
    if mode == "update":
        max_ref, planes, zbuf, ybuf, sems = rest
        max_ref[...] = jnp.full(max_ref.shape, -jnp.inf, max_ref.dtype)
    else:
        (planes, zbuf, ybuf, sems), max_ref = rest, None
    nz, nx = pad_ref.shape[0], pad_ref.shape[2]
    lanes = lax.broadcasted_iota(jnp.int32, (8, nx), 1)
    outs = list(range(width)) + list(range(nz - width, nz))
    for slot, zo in enumerate(outs):

        def load(k, rows, zo=zo):
            q = zo + k
            if q < width:
                return below_ref[q, rows, :]
            if q >= nz + width:
                return above_ref[q - nz - width, rows, :]
            return pad_ref[q - width, rows, :]

        def store(rows, value, slot=slot):
            planes[slot, rows, :] = value

        plane_blur(mode, taps_ref, load, zbuf, ybuf, lanes, store, lambda rows, zo=zo: other_ref[zo, rows, :], max_ref)
    low = pltpu.make_async_copy(planes.at[pl.ds(0, width)], volume_ref.at[pl.ds(0, width)], sems.at[0])
    high = pltpu.make_async_copy(planes.at[pl.ds(width, width)], volume_ref.at[pl.ds(nz - width, width)], sems.at[1])
    low.start()
    high.start()
    low.wait()
    high.wait()


def inner_blur(mode, width, taps, padded, other):
    nz, ny, nx = other.shape
    vmem = pltpu.VMEM
    outs = [jax.ShapeDtypeStruct((nz, ny, nx), jnp.float32)]
    out_specs = [pl.BlockSpec(memory_space=vmem)]
    if mode == "update":
        outs.append(jax.ShapeDtypeStruct((ny, nx), jnp.float32))
        out_specs.append(pl.BlockSpec(memory_space=vmem))
    elems = (nz - 2 * width) * ny * nx
    return pl.pallas_call(
        functools.partial(inner_kernel, mode, width),
        out_shape=tuple(outs),
        in_specs=[pl.BlockSpec(memory_space=pltpu.SMEM), pl.BlockSpec(memory_space=vmem), pl.BlockSpec(memory_space=vmem)],
        out_specs=tuple(out_specs),
        scratch_shapes=[pltpu.VMEM((ny + 8, nx), jnp.float32), pltpu.VMEM((ny, nx), jnp.float32)],
        compiler_params=pltpu.CompilerParams(vmem_limit_bytes=48 * 1024 * 1024),
        cost_estimate=pl.CostEstimate(flops=elems * 60, bytes_accessed=elems * 4 * 4, transcendentals=0),
    )(taps, padded, other)


def edge_blur(mode, width, taps, below, padded, above, other, volume):
    nz, ny, nx = other.shape
    vmem = pltpu.VMEM
    outs = [jax.ShapeDtypeStruct((nz, ny, nx), jnp.float32)]
    out_specs = [pl.BlockSpec(memory_space=pl.ANY)]
    if mode == "update":
        outs.append(jax.ShapeDtypeStruct((ny, nx), jnp.float32))
        out_specs.append(pl.BlockSpec(memory_space=vmem))
    elems = 2 * width * ny * nx
    return pl.pallas_call(
        functools.partial(edge_kernel, mode, width),
        out_shape=tuple(outs),
        in_specs=[pl.BlockSpec(memory_space=pltpu.SMEM)] + [pl.BlockSpec(memory_space=vmem)] * 4 + [pl.BlockSpec(memory_space=pl.ANY)],
        out_specs=tuple(out_specs),
        scratch_shapes=[
            pltpu.VMEM((2 * width, ny, nx), jnp.float32),
            pltpu.VMEM((ny + 8, nx), jnp.float32),
            pltpu.VMEM((ny, nx), jnp.float32),
            pltpu.SemaphoreType.DMA((2,)),
        ],
        input_output_aliases={5: 0},
        compiler_params=pltpu.CompilerParams(vmem_limit_bytes=48 * 1024 * 1024),
        cost_estimate=pl.CostEstimate(flops=elems * 60, bytes_accessed=elems * 4 * 4, transcendentals=0),
    )(taps, below, padded, above, other, volume)


def halo_pair(shard, axis, dim, width):
    peers, length = (lax.axis_size(axis), shard.shape[dim])
    up = [(i, (i + 1) % peers) for i in range(peers - 1)]
    down = [(j, i) for i, j in up]
    last = lax.slice_in_dim(shard, length - width, length, axis=dim)
    first = lax.slice_in_dim(shard, 0, width, axis=dim)
    before = lax.ppermute(last, axis, up)
    after = lax.ppermute(first, axis, down)
    return before, after


def split_blur(mode, taps, shard, other, width):
    ny = shard.shape[1]
    before, after = halo_pair(shard, "gy", 1, width)
    below, above = halo_pair(shard, "gz", 0, width)
    rows_padded = jnp.concatenate([before, shard, after], axis=1)
    inner = inner_blur(mode, width, taps, rows_padded, other)
    below, above, inner = lax.optimization_barrier((below, above, inner))
    gy_size = lax.axis_size("gy")
    up = [(i, i + 1) for i in range(gy_size - 1)]
    down = [(i + 1, i) for i in range(gy_size - 1)]
    last_rows = jnp.concatenate([below[:, ny - width :], above[:, ny - width :]], axis=0)
    first_rows = jnp.concatenate([below[:, :width], above[:, :width]], axis=0)
    corner_before = lax.ppermute(last_rows, "gy", up)
    corner_after = lax.ppermute(first_rows, "gy", down)
    below_padded = jnp.concatenate([corner_before[:width], below, corner_after[:width]], axis=1)
    above_padded = jnp.concatenate([corner_before[width:], above, corner_after[width:]], axis=1)
    edges = edge_blur(mode, width, taps, below_padded, rows_padded, above_padded, other, inner[0])
    if mode == "update":
        return edges[0], jnp.maximum(inner[1], edges[1])
    return edges[0]


def butterfly_max(value, axis):
    peers = lax.axis_size(axis)
    step = 1
    while step < peers:
        pairs = [(i, i ^ step) for i in range(peers)]
        value = jnp.maximum(value, lax.ppermute(value, axis, pairs))
        step *= 2
    return value


def per_device(observed, estimate, taps_z, taps_y, taps_x):
    radius = (taps_z.shape[0] - 1) // 2
    forward = jnp.concatenate([taps_z, taps_y, taps_x])
    backward = jnp.concatenate([taps_z[::-1], taps_y[::-1], taps_x[::-1]])
    ratio = split_blur("ratio", forward, estimate, observed, radius)
    updated, local_max = split_blur("update", backward, ratio, estimate, radius)
    projection = butterfly_max(local_max, "gz")
    return (updated, projection)


def solution(mesh):
    return jax.shard_map(
        per_device,
        mesh=mesh,
        in_specs=(P("gz", "gy", None), P("gz", "gy", None), P(), P(), P()),
        out_specs=(P("gz", "gy", None), P("gy", None)),
        check_vma=False,
    )
```

```python
import jax
import jax.numpy as jnp
from jax import lax
from jax.sharding import PartitionSpec as P
import functools
from jax.experimental import pallas as pl
from jax.experimental.pallas import tpu as pltpu


def plane_blur(mode, taps_ref, load, zbuf, ybuf, lanes, store, other_plane, max_ref, out_chunks=None):
    ntap = 9
    r = 4
    ny, nx = ybuf.shape
    py = ny + 2 * r
    if out_chunks is None:
        out_chunks = range(ny // 8)
    z_chunks = sorted({c for o in out_chunks for c in (o, o + 1)})
    for c in z_chunks:
        rows = pl.ds(c * 8, 8)
        acc = taps_ref[0] * load(0, rows)
        for k in range(1, ntap):
            acc = acc + taps_ref[k] * load(k, rows)
        zbuf[rows, :] = acc
    for c in out_chunks:
        acc = taps_ref[ntap] * zbuf[pl.ds(c * 8, 8), :]
        for k in range(1, ntap):
            acc = acc + taps_ref[ntap + k] * zbuf[pl.ds(c * 8 + k, 8), :]
        ybuf[pl.ds(c * 8, 8), :] = acc
    for c in out_chunks:
        rows = pl.ds(c * 8, 8)
        v = ybuf[rows, :]
        acc = None
        for k in range(ntap):
            d = k - r
            if d == 0:
                s = v
            else:
                s = pltpu.roll(v, (-d) % nx, 1)
                keep = (lanes >= -d) if d < 0 else (lanes < nx - d)
                s = jnp.where(keep, s, 0.0)
            term = taps_ref[2 * ntap + k] * s
            acc = term if acc is None else acc + term
        if mode == "ratio":
            store(rows, other_plane(rows) / acc)
        else:
            upd = other_plane(rows) * acc
            store(rows, upd)
            max_ref[rows, :] = jnp.maximum(max_ref[rows, :], upd)


def inner_kernel(mode, width, out_chunks, row_shift, taps_ref, pad_ref, other_ref, *rest):
    prev_ref = None
    if len(rest) == 5 or (mode == "ratio" and len(rest) == 4):
        prev_ref, rest = rest[0], rest[1:]
    out_ref = rest[0]
    rest = rest[1:]
    if mode == "update":
        max_ref, zbuf, ybuf = rest
        max_ref[...] = jnp.full(max_ref.shape, -jnp.inf, max_ref.dtype)
    else:
        (zbuf, ybuf), max_ref = rest, None
    nz, nx = out_ref.shape[0], out_ref.shape[2]
    lanes = lax.broadcasted_iota(jnp.int32, (8, nx), 1)

    def body(j, carry):
        zo = width + j

        def load(k, rows):
            return pad_ref[j + k, pl.ds(rows.start - row_shift, 8), :]

        def store(rows, value):
            out_ref[zo, rows, :] = value

        plane_blur(mode, taps_ref, load, zbuf, ybuf, lanes, store, lambda rows: other_ref[zo, rows, :], max_ref, out_chunks)
        if prev_ref is not None:
            for c in range(out_ref.shape[1] // 8):
                if c not in out_chunks:
                    out_ref[zo, pl.ds(c * 8, 8), :] = prev_ref[zo, pl.ds(c * 8, 8), :]
        return carry

    lax.fori_loop(0, nz - 2 * width, body, 0)


def edge_kernel(mode, width, taps_ref, below_ref, pad_ref, above_ref, other_ref, volume_in, volume_ref, *rest):
    if mode == "update":
        max_ref, planes, zbuf, ybuf, sems = rest
        max_ref[...] = jnp.full(max_ref.shape, -jnp.inf, max_ref.dtype)
    else:
        (planes, zbuf, ybuf, sems), max_ref = rest, None
    nz, nx = pad_ref.shape[0], pad_ref.shape[2]
    lanes = lax.broadcasted_iota(jnp.int32, (8, nx), 1)
    outs = list(range(width)) + list(range(nz - width, nz))
    for slot, zo in enumerate(outs):

        def load(k, rows, zo=zo):
            q = zo + k
            if q < width:
                return below_ref[q, rows, :]
            if q >= nz + width:
                return above_ref[q - nz - width, rows, :]
            return pad_ref[q - width, rows, :]

        def store(rows, value, slot=slot):
            planes[slot, rows, :] = value

        plane_blur(mode, taps_ref, load, zbuf, ybuf, lanes, store, lambda rows, zo=zo: other_ref[zo, rows, :], max_ref)
    low = pltpu.make_async_copy(planes.at[pl.ds(0, width)], volume_ref.at[pl.ds(0, width)], sems.at[0])
    high = pltpu.make_async_copy(planes.at[pl.ds(width, width)], volume_ref.at[pl.ds(nz - width, width)], sems.at[1])
    low.start()
    high.start()
    low.wait()
    high.wait()


def inner_blur(mode, width, out_chunks, row_shift, taps, padded, other, prev=None):
    nz, ny, nx = other.shape
    vmem = pltpu.VMEM
    outs = [jax.ShapeDtypeStruct((nz, ny, nx), jnp.float32)]
    out_specs = [pl.BlockSpec(memory_space=vmem)]
    if mode == "update":
        outs.append(jax.ShapeDtypeStruct((ny, nx), jnp.float32))
        out_specs.append(pl.BlockSpec(memory_space=vmem))
    operands = [taps, padded, other]
    aliases = {}
    if prev is not None:
        operands.append(prev)
    elems = (nz - 2 * width) * 8 * len(out_chunks) * nx
    return pl.pallas_call(
        functools.partial(inner_kernel, mode, width, tuple(out_chunks), row_shift),
        out_shape=tuple(outs),
        in_specs=[pl.BlockSpec(memory_space=pltpu.SMEM)] + [pl.BlockSpec(memory_space=vmem)] * (len(operands) - 1),
        out_specs=tuple(out_specs),
        scratch_shapes=[pltpu.VMEM((ny + 8, nx), jnp.float32), pltpu.VMEM((ny, nx), jnp.float32)],
        input_output_aliases=aliases,
        compiler_params=pltpu.CompilerParams(vmem_limit_bytes=48 * 1024 * 1024),
        cost_estimate=pl.CostEstimate(flops=elems * 60, bytes_accessed=elems * 4 * 4, transcendentals=0),
    )(*operands)


def edge_blur(mode, width, taps, below, padded, above, other, volume):
    nz, ny, nx = other.shape
    vmem = pltpu.VMEM
    outs = [jax.ShapeDtypeStruct((nz, ny, nx), jnp.float32)]
    out_specs = [pl.BlockSpec(memory_space=pl.ANY)]
    if mode == "update":
        outs.append(jax.ShapeDtypeStruct((ny, nx), jnp.float32))
        out_specs.append(pl.BlockSpec(memory_space=vmem))
    elems = 2 * width * ny * nx
    return pl.pallas_call(
        functools.partial(edge_kernel, mode, width),
        out_shape=tuple(outs),
        in_specs=[pl.BlockSpec(memory_space=pltpu.SMEM)] + [pl.BlockSpec(memory_space=vmem)] * 4 + [pl.BlockSpec(memory_space=pl.ANY)],
        out_specs=tuple(out_specs),
        scratch_shapes=[
            pltpu.VMEM((2 * width, ny, nx), jnp.float32),
            pltpu.VMEM((ny + 8, nx), jnp.float32),
            pltpu.VMEM((ny, nx), jnp.float32),
            pltpu.SemaphoreType.DMA((2,)),
        ],
        input_output_aliases={5: 0},
        compiler_params=pltpu.CompilerParams(vmem_limit_bytes=48 * 1024 * 1024),
        cost_estimate=pl.CostEstimate(flops=elems * 60, bytes_accessed=elems * 4 * 4, transcendentals=0),
    )(taps, below, padded, above, other, volume)


def halo_pair(shard, axis, dim, width):
    peers, length = (lax.axis_size(axis), shard.shape[dim])
    up = [(i, (i + 1) % peers) for i in range(peers - 1)]
    down = [(j, i) for i, j in up]
    last = lax.slice_in_dim(shard, length - width, length, axis=dim)
    first = lax.slice_in_dim(shard, 0, width, axis=dim)
    before = lax.ppermute(last, axis, up)
    after = lax.ppermute(first, axis, down)
    return before, after


def split_blur(mode, taps, shard, other, width):
    ny = shard.shape[1]
    chunks = ny // 8
    before, after = halo_pair(shard, "gy", 1, width)
    middle = inner_blur(mode, width, range(1, chunks - 1), width, taps, shard, other)
    before, after, middle = lax.optimization_barrier((before, after, middle))
    rows_padded = jnp.concatenate([before, shard, after], axis=1)
    below, above = halo_pair(rows_padded, "gz", 0, width)
    inner = inner_blur(mode, width, (0, chunks - 1), 0, taps, rows_padded, other, middle[0])
    edges = edge_blur(mode, width, taps, below, rows_padded, above, other, inner[0])
    if mode == "update":
        return edges[0], jnp.maximum(jnp.maximum(middle[1], inner[1]), edges[1])
    return edges[0]


def butterfly_max(value, axis):
    peers = lax.axis_size(axis)
    step = 1
    while step < peers:
        pairs = [(i, i ^ step) for i in range(peers)]
        value = jnp.maximum(value, lax.ppermute(value, axis, pairs))
        step *= 2
    return value


def per_device(observed, estimate, taps_z, taps_y, taps_x):
    radius = (taps_z.shape[0] - 1) // 2
    forward = jnp.concatenate([taps_z, taps_y, taps_x])
    backward = jnp.concatenate([taps_z[::-1], taps_y[::-1], taps_x[::-1]])
    ratio = split_blur("ratio", forward, estimate, observed, radius)
    updated, local_max = split_blur("update", backward, ratio, estimate, radius)
    projection = butterfly_max(local_max, "gz")
    return (updated, projection)


def solution(mesh):
    return jax.shard_map(
        per_device,
        mesh=mesh,
        in_specs=(P("gz", "gy", None), P("gz", "gy", None), P(), P(), P()),
        out_specs=(P("gz", "gy", None), P("gy", None)),
        check_vma=False,
    )
```

```python
import jax
import jax.numpy as jnp
from jax import lax
from jax.sharding import PartitionSpec as P
import functools
from jax.experimental import pallas as pl
from jax.experimental.pallas import tpu as pltpu


def blur_kernel(mode, segments, taps_ref, pad_ref, other_ref, out_ref, *rest):
    if mode == "update":
        max_ref, zbuf, ybuf = rest
    else:
        zbuf, ybuf = rest
    ntap = 9
    r = 4
    ny, nx = out_ref.shape[1], out_ref.shape[2]
    py = ny + 2 * r
    lanes = lax.broadcasted_iota(jnp.int32, (8, nx), 1)
    if mode == "update":
        max_ref[...] = jnp.full(max_ref.shape, -jnp.inf, max_ref.dtype)

    def plane(zo, zs, zt):
        for c in range(py // 8):
            rows = pl.ds(c * 8, 8)
            acc = taps_ref[0] * pad_ref[zs, rows, :]
            for k in range(1, ntap):
                acc = acc + taps_ref[k] * pad_ref[zs + k, rows, :]
            zbuf[rows, :] = acc
        for c in range(ny // 8):
            acc = taps_ref[ntap] * zbuf[pl.ds(c * 8, 8), :]
            for k in range(1, ntap):
                acc = acc + taps_ref[ntap + k] * zbuf[pl.ds(c * 8 + k, 8), :]
            ybuf[pl.ds(c * 8, 8), :] = acc
        for c in range(ny // 8):
            rows = pl.ds(c * 8, 8)
            v = ybuf[rows, :]
            acc = None
            for k in range(ntap):
                d = k - r
                if d == 0:
                    s = v
                else:
                    s = pltpu.roll(v, (-d) % nx, 1)
                    keep = (lanes >= -d) if d < 0 else (lanes < nx - d)
                    s = jnp.where(keep, s, 0.0)
                term = taps_ref[2 * ntap + k] * s
                acc = term if acc is None else acc + term
            if mode == "ratio":
                out_ref[zo, rows, :] = other_ref[zt, rows, :] / acc
            else:
                upd = other_ref[zt, rows, :] * acc
                out_ref[zo, rows, :] = upd
                max_ref[rows, :] = jnp.maximum(max_ref[rows, :], upd)

    for out_start, count, src_start, other_start in segments:
        def body(j, carry, out_start=out_start, src_start=src_start, other_start=other_start):
            plane(out_start + j, src_start + j, other_start + j)
            return carry

        lax.fori_loop(0, count, body, 0)


def fused_blur(mode, segments, taps, padded, other):
    nzo = sum(seg[1] for seg in segments)
    ny, nx = other.shape[1], other.shape[2]
    vmem = pltpu.VMEM
    outs = [jax.ShapeDtypeStruct((nzo, ny, nx), jnp.float32)]
    out_specs = [pl.BlockSpec(memory_space=vmem)]
    if mode == "update":
        outs.append(jax.ShapeDtypeStruct((ny, nx), jnp.float32))
        out_specs.append(pl.BlockSpec(memory_space=vmem))
    elems = nzo * ny * nx
    return pl.pallas_call(
        functools.partial(blur_kernel, mode, tuple(segments)),
        out_shape=tuple(outs),
        in_specs=[pl.BlockSpec(memory_space=pltpu.SMEM), pl.BlockSpec(memory_space=vmem), pl.BlockSpec(memory_space=vmem)],
        out_specs=tuple(out_specs),
        scratch_shapes=[pltpu.VMEM((ny + 8, nx), jnp.float32), pltpu.VMEM((ny, nx), jnp.float32)],
        compiler_params=pltpu.CompilerParams(vmem_limit_bytes=48 * 1024 * 1024),
        cost_estimate=pl.CostEstimate(flops=elems * 60, bytes_accessed=elems * 4 * 4, transcendentals=0),
    )(taps, padded, other)


def halo_pair(shard, axis, dim, width):
    peers, length = (lax.axis_size(axis), shard.shape[dim])
    up = [(i, (i + 1) % peers) for i in range(peers - 1)]
    down = [(j, i) for i, j in up]
    last = lax.slice_in_dim(shard, length - width, length, axis=dim)
    first = lax.slice_in_dim(shard, 0, width, axis=dim)
    before = lax.ppermute(last, axis, up)
    after = lax.ppermute(first, axis, down)
    return before, after


def split_blur(mode, taps, shard, other, width):
    nz = shard.shape[0]
    before, after = halo_pair(shard, "gy", 1, width)
    rows_padded = jnp.concatenate([before, shard, after], axis=1)
    below, above = halo_pair(rows_padded, "gz", 0, width)
    inner = fused_blur(mode, [(0, nz - 2 * width, 0, width)], taps, rows_padded, other)
    low_slab = jnp.concatenate([below, rows_padded[: 2 * width]], axis=0)
    high_slab = jnp.concatenate([rows_padded[nz - 2 * width :], above], axis=0)
    low = fused_blur(mode, [(0, width, 0, 0)], taps, low_slab, other)
    high = fused_blur(mode, [(0, width, 0, nz - width)], taps, high_slab, other)
    volume = jnp.concatenate([low[0], inner[0], high[0]], axis=0)
    if mode == "update":
        return volume, jnp.maximum(jnp.maximum(inner[1], low[1]), high[1])
    return volume


def butterfly_max(value, axis):
    peers = lax.axis_size(axis)
    step = 1
    while step < peers:
        pairs = [(i, i ^ step) for i in range(peers)]
        value = jnp.maximum(value, lax.ppermute(value, axis, pairs))
        step *= 2
    return value


def per_device(observed, estimate, taps_z, taps_y, taps_x):
    radius = (taps_z.shape[0] - 1) // 2
    forward = jnp.concatenate([taps_z, taps_y, taps_x])
    backward = jnp.concatenate([taps_z[::-1], taps_y[::-1], taps_x[::-1]])
    ratio = split_blur("ratio", forward, estimate, observed, radius)
    updated, local_max = split_blur("update", backward, ratio, estimate, radius)
    projection = butterfly_max(local_max, "gz")
    return (updated, projection)


def solution(mesh):
    return jax.shard_map(
        per_device,
        mesh=mesh,
        in_specs=(P("gz", "gy", None), P("gz", "gy", None), P(), P(), P()),
        out_specs=(P("gz", "gy", None), P("gy", None)),
        check_vma=False,
    )
```

```python
import jax
import jax.numpy as jnp
from jax import lax
from jax.sharding import PartitionSpec as P
import functools
from jax.experimental import pallas as pl
from jax.experimental.pallas import tpu as pltpu


def blur_kernel(mode, segments, taps_ref, pad_ref, other_ref, out_ref, *rest):
    if mode == "update":
        max_ref, zbuf, ybuf = rest
    else:
        zbuf, ybuf = rest
    ntap = 9
    r = 4
    ny, nx = out_ref.shape[1], out_ref.shape[2]
    py = ny + 2 * r
    lanes = lax.broadcasted_iota(jnp.int32, (8, nx), 1)
    if mode == "update":
        max_ref[...] = jnp.full(max_ref.shape, -jnp.inf, max_ref.dtype)

    def plane(zo, zs, zt):
        for c in range(py // 8):
            rows = pl.ds(c * 8, 8)
            acc = taps_ref[0] * pad_ref[zs, rows, :]
            for k in range(1, ntap):
                acc = acc + taps_ref[k] * pad_ref[zs + k, rows, :]
            zbuf[rows, :] = acc
        for c in range(ny // 8):
            acc = taps_ref[ntap] * zbuf[pl.ds(c * 8, 8), :]
            for k in range(1, ntap):
                acc = acc + taps_ref[ntap + k] * zbuf[pl.ds(c * 8 + k, 8), :]
            ybuf[pl.ds(c * 8, 8), :] = acc
        for c in range(ny // 8):
            rows = pl.ds(c * 8, 8)
            v = ybuf[rows, :]
            acc = None
            for k in range(ntap):
                d = k - r
                if d == 0:
                    s = v
                else:
                    s = pltpu.roll(v, (-d) % nx, 1)
                    keep = (lanes >= -d) if d < 0 else (lanes < nx - d)
                    s = jnp.where(keep, s, 0.0)
                term = taps_ref[2 * ntap + k] * s
                acc = term if acc is None else acc + term
            if mode == "ratio":
                out_ref[zo, rows, :] = other_ref[zt, rows, :] / acc
            else:
                upd = other_ref[zt, rows, :] * acc
                out_ref[zo, rows, :] = upd
                max_ref[rows, :] = jnp.maximum(max_ref[rows, :], upd)

    for out_start, count, src_start, other_start in segments:
        def body(j, carry, out_start=out_start, src_start=src_start, other_start=other_start):
            plane(out_start + j, src_start + j, other_start + j)
            return carry

        lax.fori_loop(0, count, body, 0)


def fused_blur(mode, segments, taps, padded, other):
    nzo = sum(seg[1] for seg in segments)
    ny, nx = other.shape[1], other.shape[2]
    vmem = pltpu.VMEM
    outs = [jax.ShapeDtypeStruct((nzo, ny, nx), jnp.float32)]
    out_specs = [pl.BlockSpec(memory_space=vmem)]
    if mode == "update":
        outs.append(jax.ShapeDtypeStruct((ny, nx), jnp.float32))
        out_specs.append(pl.BlockSpec(memory_space=vmem))
    elems = nzo * ny * nx
    return pl.pallas_call(
        functools.partial(blur_kernel, mode, tuple(segments)),
        out_shape=tuple(outs),
        in_specs=[pl.BlockSpec(memory_space=pltpu.SMEM), pl.BlockSpec(memory_space=vmem), pl.BlockSpec(memory_space=vmem)],
        out_specs=tuple(out_specs),
        scratch_shapes=[pltpu.VMEM((ny + 8, nx), jnp.float32), pltpu.VMEM((ny, nx), jnp.float32)],
        compiler_params=pltpu.CompilerParams(vmem_limit_bytes=48 * 1024 * 1024),
        cost_estimate=pl.CostEstimate(flops=elems * 60, bytes_accessed=elems * 4 * 4, transcendentals=0),
    )(taps, padded, other)


def halo_pair(shard, axis, dim, width):
    peers, length = (lax.axis_size(axis), shard.shape[dim])
    up = [(i, (i + 1) % peers) for i in range(peers - 1)]
    down = [(j, i) for i, j in up]
    last = lax.slice_in_dim(shard, length - width, length, axis=dim)
    first = lax.slice_in_dim(shard, 0, width, axis=dim)
    before = lax.ppermute(last, axis, up)
    after = lax.ppermute(first, axis, down)
    return before, after


def split_blur(mode, taps, shard, other, width):
    nz = shard.shape[0]
    before, after = halo_pair(shard, "gy", 1, width)
    rows_padded = jnp.concatenate([before, shard, after], axis=1)
    below, above = halo_pair(rows_padded, "gz", 0, width)
    inner = fused_blur(mode, [(0, nz - 2 * width, 0, width)], taps, rows_padded, other)
    low_slab = jnp.concatenate([below, rows_padded[: 2 * width]], axis=0)
    low = fused_blur(mode, [(0, width, 0, 0)], taps, low_slab, other)
    above, low = lax.optimization_barrier((above, low))
    high_slab = jnp.concatenate([rows_padded[nz - 2 * width :], above], axis=0)
    high = fused_blur(mode, [(0, width, 0, nz - width)], taps, high_slab, other)
    volume = jnp.concatenate([low[0], inner[0], high[0]], axis=0)
    if mode == "update":
        return volume, jnp.maximum(jnp.maximum(inner[1], low[1]), high[1])
    return volume


def butterfly_max(value, axis):
    peers = lax.axis_size(axis)
    step = 1
    while step < peers:
        pairs = [(i, i ^ step) for i in range(peers)]
        value = jnp.maximum(value, lax.ppermute(value, axis, pairs))
        step *= 2
    return value


def per_device(observed, estimate, taps_z, taps_y, taps_x):
    radius = (taps_z.shape[0] - 1) // 2
    forward = jnp.concatenate([taps_z, taps_y, taps_x])
    backward = jnp.concatenate([taps_z[::-1], taps_y[::-1], taps_x[::-1]])
    ratio = split_blur("ratio", forward, estimate, observed, radius)
    updated, local_max = split_blur("update", backward, ratio, estimate, radius)
    projection = butterfly_max(local_max, "gz")
    return (updated, projection)


def solution(mesh):
    return jax.shard_map(
        per_device,
        mesh=mesh,
        in_specs=(P("gz", "gy", None), P("gz", "gy", None), P(), P(), P()),
        out_specs=(P("gz", "gy", None), P("gy", None)),
        check_vma=False,
    )
```

```python
import jax
import jax.numpy as jnp
from jax import lax
from jax.sharding import PartitionSpec as P
import functools
from jax.experimental import pallas as pl
from jax.experimental.pallas import tpu as pltpu


def blur_kernel(mode, segments, taps_ref, pad_ref, other_ref, out_ref, *rest):
    if mode == "update":
        max_ref, zbuf, ybuf = rest
    else:
        zbuf, ybuf = rest
    ntap = 9
    r = 4
    ny, nx = out_ref.shape[1], out_ref.shape[2]
    py = ny + 2 * r
    lanes = lax.broadcasted_iota(jnp.int32, (8, nx), 1)
    if mode == "update":
        max_ref[...] = jnp.full(max_ref.shape, -jnp.inf, max_ref.dtype)

    def plane(zo, zs, zt):
        for c in range(py // 8):
            rows = pl.ds(c * 8, 8)
            acc = taps_ref[0] * pad_ref[zs, rows, :]
            for k in range(1, ntap):
                acc = acc + taps_ref[k] * pad_ref[zs + k, rows, :]
            zbuf[rows, :] = acc
        for c in range(ny // 8):
            acc = taps_ref[ntap] * zbuf[pl.ds(c * 8, 8), :]
            for k in range(1, ntap):
                acc = acc + taps_ref[ntap + k] * zbuf[pl.ds(c * 8 + k, 8), :]
            ybuf[pl.ds(c * 8, 8), :] = acc
        for c in range(ny // 8):
            rows = pl.ds(c * 8, 8)
            v = ybuf[rows, :]
            acc = None
            for k in range(ntap):
                d = k - r
                if d == 0:
                    s = v
                else:
                    s = pltpu.roll(v, (-d) % nx, 1)
                    keep = (lanes >= -d) if d < 0 else (lanes < nx - d)
                    s = jnp.where(keep, s, 0.0)
                term = taps_ref[2 * ntap + k] * s
                acc = term if acc is None else acc + term
            if mode == "ratio":
                out_ref[zo, rows, :] = other_ref[zt, rows, :] / acc
            else:
                upd = other_ref[zt, rows, :] * acc
                out_ref[zo, rows, :] = upd
                max_ref[rows, :] = jnp.maximum(max_ref[rows, :], upd)

    for out_start, count, src_start, other_start in segments:
        def body(j, carry, out_start=out_start, src_start=src_start, other_start=other_start):
            plane(out_start + j, src_start + j, other_start + j)
            return carry

        lax.fori_loop(0, count, body, 0)


def fused_blur(mode, segments, taps, padded, other):
    nzo = sum(seg[1] for seg in segments)
    ny, nx = other.shape[1], other.shape[2]
    vmem = pltpu.VMEM
    outs = [jax.ShapeDtypeStruct((nzo, ny, nx), jnp.float32)]
    out_specs = [pl.BlockSpec(memory_space=vmem)]
    if mode == "update":
        outs.append(jax.ShapeDtypeStruct((ny, nx), jnp.float32))
        out_specs.append(pl.BlockSpec(memory_space=vmem))
    elems = nzo * ny * nx
    return pl.pallas_call(
        functools.partial(blur_kernel, mode, tuple(segments)),
        out_shape=tuple(outs),
        in_specs=[pl.BlockSpec(memory_space=pltpu.SMEM), pl.BlockSpec(memory_space=vmem), pl.BlockSpec(memory_space=vmem)],
        out_specs=tuple(out_specs),
        scratch_shapes=[pltpu.VMEM((ny + 8, nx), jnp.float32), pltpu.VMEM((ny, nx), jnp.float32)],
        compiler_params=pltpu.CompilerParams(vmem_limit_bytes=48 * 1024 * 1024),
        cost_estimate=pl.CostEstimate(flops=elems * 60, bytes_accessed=elems * 4 * 4, transcendentals=0),
    )(taps, padded, other)


def halo_pair(shard, axis, dim, width):
    peers, length = (lax.axis_size(axis), shard.shape[dim])
    up = [(i, (i + 1) % peers) for i in range(peers - 1)]
    down = [(j, i) for i, j in up]
    last = lax.slice_in_dim(shard, length - width, length, axis=dim)
    first = lax.slice_in_dim(shard, 0, width, axis=dim)
    before = lax.ppermute(last, axis, up)
    after = lax.ppermute(first, axis, down)
    return before, after


def split_blur(mode, taps, shard, other, width):
    nz = shard.shape[0]
    before, after = halo_pair(shard, "gy", 1, width)
    rows_padded = jnp.concatenate([before, shard, after], axis=1)
    below, above = halo_pair(rows_padded, "gz", 0, width)
    inner = fused_blur(mode, [(0, nz - 2 * width, 0, width)], taps, rows_padded, other)
    low_slab = jnp.concatenate([below, rows_padded[: 2 * width]], axis=0)
    high_slab = jnp.concatenate([rows_padded[nz - 2 * width :], above], axis=0)
    low = fused_blur(mode, [(0, width, 0, 0)], taps, low_slab, other)
    high = fused_blur(mode, [(0, width, 0, nz - width)], taps, high_slab, other)
    volume = jnp.concatenate([low[0], inner[0], high[0]], axis=0)
    if mode == "update":
        return volume, jnp.maximum(jnp.maximum(inner[1], low[1]), high[1])
    return volume


def butterfly_max(value, axis):
    peers = lax.axis_size(axis)
    step = peers // 2
    while step >= 1:
        pairs = [(i, i ^ step) for i in range(peers)]
        value = jnp.maximum(value, lax.ppermute(value, axis, pairs))
        step //= 2
    return value


def per_device(observed, estimate, taps_z, taps_y, taps_x):
    radius = (taps_z.shape[0] - 1) // 2
    forward = jnp.concatenate([taps_z, taps_y, taps_x])
    backward = jnp.concatenate([taps_z[::-1], taps_y[::-1], taps_x[::-1]])
    ratio = split_blur("ratio", forward, estimate, observed, radius)
    updated, local_max = split_blur("update", backward, ratio, estimate, radius)
    projection = butterfly_max(local_max, "gz")
    return (updated, projection)


def solution(mesh):
    return jax.shard_map(
        per_device,
        mesh=mesh,
        in_specs=(P("gz", "gy", None), P("gz", "gy", None), P(), P(), P()),
        out_specs=(P("gz", "gy", None), P("gy", None)),
        check_vma=False,
    )
```

```python
import jax
import jax.numpy as jnp
from jax import lax
from jax.sharding import PartitionSpec as P
import functools
from jax.experimental import pallas as pl
from jax.experimental.pallas import tpu as pltpu


def blur_kernel(mode, segments, taps_ref, pad_ref, other_ref, out_ref, *rest):
    if mode == "update":
        max_ref, zbuf, ybuf = rest
    else:
        zbuf, ybuf = rest
    ntap = 9
    r = 4
    ny, nx = out_ref.shape[1], out_ref.shape[2]
    py = ny + 2 * r
    lanes = lax.broadcasted_iota(jnp.int32, (8, nx), 1)
    if mode == "update":
        max_ref[...] = jnp.full(max_ref.shape, -jnp.inf, max_ref.dtype)

    def plane(zo, zs, zt):
        for c in range(py // 8):
            rows = pl.ds(c * 8, 8)
            acc = taps_ref[0] * pad_ref[zs, rows, :]
            for k in range(1, ntap):
                acc = acc + taps_ref[k] * pad_ref[zs + k, rows, :]
            zbuf[rows, :] = acc
        for c in range(ny // 8):
            acc = taps_ref[ntap] * zbuf[pl.ds(c * 8, 8), :]
            for k in range(1, ntap):
                acc = acc + taps_ref[ntap + k] * zbuf[pl.ds(c * 8 + k, 8), :]
            ybuf[pl.ds(c * 8, 8), :] = acc
        for c in range(ny // 8):
            rows = pl.ds(c * 8, 8)
            v = ybuf[rows, :]
            acc = None
            for k in range(ntap):
                d = k - r
                if d == 0:
                    s = v
                else:
                    s = pltpu.roll(v, (-d) % nx, 1)
                    keep = (lanes >= -d) if d < 0 else (lanes < nx - d)
                    s = jnp.where(keep, s, 0.0)
                term = taps_ref[2 * ntap + k] * s
                acc = term if acc is None else acc + term
            if mode == "ratio":
                out_ref[zo, rows, :] = other_ref[zt, rows, :] / acc
            else:
                upd = other_ref[zt, rows, :] * acc
                out_ref[zo, rows, :] = upd
                max_ref[rows, :] = jnp.maximum(max_ref[rows, :], upd)

    for out_start, count, src_start, other_start in segments:
        def body(j, carry, out_start=out_start, src_start=src_start, other_start=other_start):
            plane(out_start + j, src_start + j, other_start + j)
            return carry

        lax.fori_loop(0, count, body, 0)


def fused_blur(mode, segments, taps, padded, other):
    nzo = sum(seg[1] for seg in segments)
    ny, nx = other.shape[1], other.shape[2]
    vmem = pltpu.VMEM
    outs = [jax.ShapeDtypeStruct((nzo, ny, nx), jnp.float32)]
    out_specs = [pl.BlockSpec(memory_space=vmem)]
    if mode == "update":
        outs.append(jax.ShapeDtypeStruct((ny, nx), jnp.float32))
        out_specs.append(pl.BlockSpec(memory_space=vmem))
    elems = nzo * ny * nx
    return pl.pallas_call(
        functools.partial(blur_kernel, mode, tuple(segments)),
        out_shape=tuple(outs),
        in_specs=[pl.BlockSpec(memory_space=pltpu.SMEM), pl.BlockSpec(memory_space=vmem), pl.BlockSpec(memory_space=vmem)],
        out_specs=tuple(out_specs),
        scratch_shapes=[pltpu.VMEM((ny + 8, nx), jnp.float32), pltpu.VMEM((ny, nx), jnp.float32)],
        compiler_params=pltpu.CompilerParams(vmem_limit_bytes=48 * 1024 * 1024),
        cost_estimate=pl.CostEstimate(flops=elems * 60, bytes_accessed=elems * 4 * 4, transcendentals=0),
    )(taps, padded, other)


def halo_pair(shard, axis, dim, width):
    peers, length = (lax.axis_size(axis), shard.shape[dim])
    up = [(i, (i + 1) % peers) for i in range(peers - 1)]
    down = [(j, i) for i, j in up]
    last = lax.slice_in_dim(shard, length - width, length, axis=dim)
    first = lax.slice_in_dim(shard, 0, width, axis=dim)
    before = lax.ppermute(last, axis, up)
    after = lax.ppermute(first, axis, down)
    return before, after


def split_blur(mode, taps, shard, other, width):
    nz = shard.shape[0]
    before, after = halo_pair(shard, "gy", 1, width)
    peers = lax.axis_size("gz")
    up = [(i, i + 1) for i in range(peers - 1)]
    down = [(i + 1, i) for i in range(peers - 1)]
    first = jnp.concatenate([before[:width], shard[:width], after[:width]], axis=1)
    last = jnp.concatenate([before[nz - width :], shard[nz - width :], after[nz - width :]], axis=1)
    below = lax.ppermute(last, "gz", up)
    above = lax.ppermute(first, "gz", down)
    rows_padded = jnp.concatenate([before, shard, after], axis=1)
    inner = fused_blur(mode, [(0, nz - 2 * width, 0, width)], taps, rows_padded, other)
    low_slab = jnp.concatenate([below, rows_padded[: 2 * width]], axis=0)
    high_slab = jnp.concatenate([rows_padded[nz - 2 * width :], above], axis=0)
    low = fused_blur(mode, [(0, width, 0, 0)], taps, low_slab, other)
    high = fused_blur(mode, [(0, width, 0, nz - width)], taps, high_slab, other)
    volume = jnp.concatenate([low[0], inner[0], high[0]], axis=0)
    if mode == "update":
        return volume, jnp.maximum(jnp.maximum(inner[1], low[1]), high[1])
    return volume


def butterfly_max(value, axis):
    peers = lax.axis_size(axis)
    step = peers // 2
    while step >= 1:
        pairs = [(i, i ^ step) for i in range(peers)]
        value = jnp.maximum(value, lax.ppermute(value, axis, pairs))
        step //= 2
    return value


def per_device(observed, estimate, taps_z, taps_y, taps_x):
    radius = (taps_z.shape[0] - 1) // 2
    forward = jnp.concatenate([taps_z, taps_y, taps_x])
    backward = jnp.concatenate([taps_z[::-1], taps_y[::-1], taps_x[::-1]])
    ratio = split_blur("ratio", forward, estimate, observed, radius)
    updated, local_max = split_blur("update", backward, ratio, estimate, radius)
    projection = butterfly_max(local_max, "gz")
    return (updated, projection)


def solution(mesh):
    return jax.shard_map(
        per_device,
        mesh=mesh,
        in_specs=(P("gz", "gy", None), P("gz", "gy", None), P(), P(), P()),
        out_specs=(P("gz", "gy", None), P("gy", None)),
        check_vma=False,
    )
```

```python
import jax
import jax.numpy as jnp
from jax import lax
from jax.sharding import PartitionSpec as P
import functools
from jax.experimental import pallas as pl
from jax.experimental.pallas import tpu as pltpu


def blur_kernel(mode, segments, taps_ref, pad_ref, other_ref, out_ref, *rest):
    if mode == "update":
        max_ref, zbuf, ybuf = rest
    else:
        zbuf, ybuf = rest
    ntap = 9
    r = 4
    ny, nx = out_ref.shape[1], out_ref.shape[2]
    py = ny + 2 * r
    lanes = lax.broadcasted_iota(jnp.int32, (8, nx), 1)
    if mode == "update":
        max_ref[...] = jnp.full(max_ref.shape, -jnp.inf, max_ref.dtype)

    def plane(zo, zs, zt):
        for c in range(py // 8):
            rows = pl.ds(c * 8, 8)
            acc = taps_ref[0] * pad_ref[zs, rows, :]
            for k in range(1, ntap):
                acc = acc + taps_ref[k] * pad_ref[zs + k, rows, :]
            zbuf[rows, :] = acc
        for c in range(ny // 8):
            acc = taps_ref[ntap] * zbuf[pl.ds(c * 8, 8), :]
            for k in range(1, ntap):
                acc = acc + taps_ref[ntap + k] * zbuf[pl.ds(c * 8 + k, 8), :]
            ybuf[pl.ds(c * 8, 8), :] = acc
        for c in range(ny // 8):
            rows = pl.ds(c * 8, 8)
            v = ybuf[rows, :]
            acc = None
            for k in range(ntap):
                d = k - r
                if d == 0:
                    s = v
                else:
                    s = pltpu.roll(v, (-d) % nx, 1)
                    keep = (lanes >= -d) if d < 0 else (lanes < nx - d)
                    s = jnp.where(keep, s, 0.0)
                term = taps_ref[2 * ntap + k] * s
                acc = term if acc is None else acc + term
            if mode == "ratio":
                out_ref[zo, rows, :] = other_ref[zt, rows, :] / acc
            else:
                upd = other_ref[zt, rows, :] * acc
                out_ref[zo, rows, :] = upd
                max_ref[rows, :] = jnp.maximum(max_ref[rows, :], upd)

    for out_start, count, src_start, other_start in segments:
        def body(j, carry, out_start=out_start, src_start=src_start, other_start=other_start):
            plane(out_start + j, src_start + j, other_start + j)
            return carry

        lax.fori_loop(0, count, body, 0)


def fused_blur(mode, segments, taps, padded, other):
    nzo = sum(seg[1] for seg in segments)
    ny, nx = other.shape[1], other.shape[2]
    vmem = pltpu.VMEM
    outs = [jax.ShapeDtypeStruct((nzo, ny, nx), jnp.float32)]
    out_specs = [pl.BlockSpec(memory_space=vmem)]
    if mode == "update":
        outs.append(jax.ShapeDtypeStruct((ny, nx), jnp.float32))
        out_specs.append(pl.BlockSpec(memory_space=vmem))
    elems = nzo * ny * nx
    return pl.pallas_call(
        functools.partial(blur_kernel, mode, tuple(segments)),
        out_shape=tuple(outs),
        in_specs=[pl.BlockSpec(memory_space=pltpu.SMEM), pl.BlockSpec(memory_space=vmem), pl.BlockSpec(memory_space=vmem)],
        out_specs=tuple(out_specs),
        scratch_shapes=[pltpu.VMEM((ny + 8, nx), jnp.float32), pltpu.VMEM((ny, nx), jnp.float32)],
        compiler_params=pltpu.CompilerParams(vmem_limit_bytes=48 * 1024 * 1024),
        cost_estimate=pl.CostEstimate(flops=elems * 60, bytes_accessed=elems * 4 * 4, transcendentals=0),
    )(taps, padded, other)


def halo_pair(shard, axis, dim, width):
    peers, length = (lax.axis_size(axis), shard.shape[dim])
    up = [(i, (i + 1) % peers) for i in range(peers - 1)]
    down = [(j, i) for i, j in up]
    last = lax.slice_in_dim(shard, length - width, length, axis=dim)
    first = lax.slice_in_dim(shard, 0, width, axis=dim)
    before = lax.ppermute(last, axis, up)
    after = lax.ppermute(first, axis, down)
    return before, after


def split_blur(mode, taps, shard, other, width):
    nz = shard.shape[0]
    before, after = halo_pair(shard, "gy", 1, width)
    rows_padded = jnp.concatenate([before, shard, after], axis=1)
    below, above = halo_pair(rows_padded, "gz", 0, width)
    inner = fused_blur(mode, [(0, nz - 2 * width, 0, width)], taps, rows_padded, other)
    low_slab = jnp.concatenate([below, rows_padded[: 2 * width]], axis=0)
    high_slab = jnp.concatenate([rows_padded[nz - 2 * width :], above], axis=0)
    low = fused_blur(mode, [(0, width, 0, 0)], taps, low_slab, other[:width])
    high = fused_blur(mode, [(0, width, 0, 0)], taps, high_slab, other[nz - width :])
    volume = jnp.concatenate([low[0], inner[0], high[0]], axis=0)
    if mode == "update":
        return volume, jnp.maximum(jnp.maximum(inner[1], low[1]), high[1])
    return volume


def butterfly_max(value, axis):
    peers = lax.axis_size(axis)
    step = peers // 2
    while step >= 1:
        pairs = [(i, i ^ step) for i in range(peers)]
        value = jnp.maximum(value, lax.ppermute(value, axis, pairs))
        step //= 2
    return value


def per_device(observed, estimate, taps_z, taps_y, taps_x):
    radius = (taps_z.shape[0] - 1) // 2
    forward = jnp.concatenate([taps_z, taps_y, taps_x])
    backward = jnp.concatenate([taps_z[::-1], taps_y[::-1], taps_x[::-1]])
    ratio = split_blur("ratio", forward, estimate, observed, radius)
    updated, local_max = split_blur("update", backward, ratio, estimate, radius)
    projection = butterfly_max(local_max, "gz")
    return (updated, projection)


def solution(mesh):
    return jax.shard_map(
        per_device,
        mesh=mesh,
        in_specs=(P("gz", "gy", None), P("gz", "gy", None), P(), P(), P()),
        out_specs=(P("gz", "gy", None), P("gy", None)),
        check_vma=False,
    )
```

```python
import jax
import jax.numpy as jnp
from jax import lax
from jax.sharding import PartitionSpec as P
import functools
from jax.experimental import pallas as pl
from jax.experimental.pallas import tpu as pltpu


def blur_kernel(mode, segments, taps_ref, pad_ref, other_ref, out_ref, *rest):
    if mode == "update":
        max_ref, zbuf, ybuf = rest
    else:
        zbuf, ybuf = rest
    ntap = 9
    r = 4
    ny, nx = out_ref.shape[1], out_ref.shape[2]
    py = ny + 2 * r
    lanes = lax.broadcasted_iota(jnp.int32, (8, nx), 1)
    if mode == "update":
        max_ref[...] = jnp.full(max_ref.shape, -jnp.inf, max_ref.dtype)

    def plane(zo, zs, zt):
        for c in range(py // 8):
            rows = pl.ds(c * 8, 8)
            acc = taps_ref[0] * pad_ref[zs, rows, :]
            for k in range(1, ntap):
                acc = acc + taps_ref[k] * pad_ref[zs + k, rows, :]
            zbuf[rows, :] = acc
        for c in range(ny // 8):
            acc = taps_ref[ntap] * zbuf[pl.ds(c * 8, 8), :]
            for k in range(1, ntap):
                acc = acc + taps_ref[ntap + k] * zbuf[pl.ds(c * 8 + k, 8), :]
            ybuf[pl.ds(c * 8, 8), :] = acc
        for c in range(ny // 8):
            rows = pl.ds(c * 8, 8)
            v = ybuf[rows, :]
            acc = None
            for k in range(ntap):
                d = k - r
                if d == 0:
                    s = v
                else:
                    s = pltpu.roll(v, (-d) % nx, 1)
                    keep = (lanes >= -d) if d < 0 else (lanes < nx - d)
                    s = jnp.where(keep, s, 0.0)
                term = taps_ref[2 * ntap + k] * s
                acc = term if acc is None else acc + term
            if mode == "ratio":
                out_ref[zo, rows, :] = other_ref[zt, rows, :] / acc
            else:
                upd = other_ref[zt, rows, :] * acc
                out_ref[zo, rows, :] = upd
                max_ref[rows, :] = jnp.maximum(max_ref[rows, :], upd)

    for out_start, count, src_start, other_start in segments:
        def body(j, carry, out_start=out_start, src_start=src_start, other_start=other_start):
            plane(out_start + j, src_start + j, other_start + j)
            return carry

        lax.fori_loop(0, count, body, 0)


def fused_blur(mode, segments, taps, padded, other):
    nzo = sum(seg[1] for seg in segments)
    ny, nx = other.shape[1], other.shape[2]
    vmem = pltpu.VMEM
    outs = [jax.ShapeDtypeStruct((nzo, ny, nx), jnp.float32)]
    out_specs = [pl.BlockSpec(memory_space=vmem)]
    if mode == "update":
        outs.append(jax.ShapeDtypeStruct((ny, nx), jnp.float32))
        out_specs.append(pl.BlockSpec(memory_space=vmem))
    elems = nzo * ny * nx
    return pl.pallas_call(
        functools.partial(blur_kernel, mode, tuple(segments)),
        out_shape=tuple(outs),
        in_specs=[pl.BlockSpec(memory_space=pltpu.SMEM), pl.BlockSpec(memory_space=vmem), pl.BlockSpec(memory_space=vmem)],
        out_specs=tuple(out_specs),
        scratch_shapes=[pltpu.VMEM((ny + 8, nx), jnp.float32), pltpu.VMEM((ny, nx), jnp.float32)],
        compiler_params=pltpu.CompilerParams(vmem_limit_bytes=48 * 1024 * 1024),
        cost_estimate=pl.CostEstimate(flops=elems * 60, bytes_accessed=elems * 4 * 4, transcendentals=0),
    )(taps, padded, other)


def edge_kernel(mode, width, halo_first, taps_ref, halo_ref, own_ref, other_ref, out_ref, *rest):
    if mode == "update":
        max_ref, zbuf, ybuf = rest
        max_ref[...] = jnp.full(max_ref.shape, -jnp.inf, max_ref.dtype)
    else:
        (zbuf, ybuf), max_ref = rest, None
    ntap = 9
    r = 4
    ny, nx = out_ref.shape[1], out_ref.shape[2]
    py = ny + 2 * r
    lanes = lax.broadcasted_iota(jnp.int32, (8, nx), 1)
    for zo in range(width):

        def load(q, rows):
            if halo_first:
                return halo_ref[q, rows, :] if q < width else own_ref[q - width, rows, :]
            return own_ref[q, rows, :] if q < 2 * width else halo_ref[q - 2 * width, rows, :]

        for c in range(py // 8):
            rows = pl.ds(c * 8, 8)
            acc = taps_ref[0] * load(zo, rows)
            for k in range(1, ntap):
                acc = acc + taps_ref[k] * load(zo + k, rows)
            zbuf[rows, :] = acc
        for c in range(ny // 8):
            acc = taps_ref[ntap] * zbuf[pl.ds(c * 8, 8), :]
            for k in range(1, ntap):
                acc = acc + taps_ref[ntap + k] * zbuf[pl.ds(c * 8 + k, 8), :]
            ybuf[pl.ds(c * 8, 8), :] = acc
        for c in range(ny // 8):
            rows = pl.ds(c * 8, 8)
            v = ybuf[rows, :]
            acc = None
            for k in range(ntap):
                d = k - r
                if d == 0:
                    t = v
                else:
                    t = pltpu.roll(v, (-d) % nx, 1)
                    keep = (lanes >= -d) if d < 0 else (lanes < nx - d)
                    t = jnp.where(keep, t, 0.0)
                term = taps_ref[2 * ntap + k] * t
                acc = term if acc is None else acc + term
            if mode == "ratio":
                out_ref[zo, rows, :] = other_ref[zo, rows, :] / acc
            else:
                upd = other_ref[zo, rows, :] * acc
                out_ref[zo, rows, :] = upd
                max_ref[rows, :] = jnp.maximum(max_ref[rows, :], upd)


def edge_blur(mode, width, halo_first, taps, halo, own, other):
    nzo, ny, nx = other.shape
    vmem = pltpu.VMEM
    outs = [jax.ShapeDtypeStruct((nzo, ny, nx), jnp.float32)]
    out_specs = [pl.BlockSpec(memory_space=vmem)]
    if mode == "update":
        outs.append(jax.ShapeDtypeStruct((ny, nx), jnp.float32))
        out_specs.append(pl.BlockSpec(memory_space=vmem))
    elems = nzo * ny * nx
    return pl.pallas_call(
        functools.partial(edge_kernel, mode, width, halo_first),
        out_shape=tuple(outs),
        in_specs=[pl.BlockSpec(memory_space=pltpu.SMEM)] + [pl.BlockSpec(memory_space=vmem)] * 3,
        out_specs=tuple(out_specs),
        scratch_shapes=[pltpu.VMEM((ny + 8, nx), jnp.float32), pltpu.VMEM((ny, nx), jnp.float32)],
        compiler_params=pltpu.CompilerParams(vmem_limit_bytes=48 * 1024 * 1024),
        cost_estimate=pl.CostEstimate(flops=elems * 60, bytes_accessed=elems * 4 * 4, transcendentals=0),
    )(taps, halo, own, other)


def halo_pair(shard, axis, dim, width):
    peers, length = (lax.axis_size(axis), shard.shape[dim])
    up = [(i, (i + 1) % peers) for i in range(peers - 1)]
    down = [(j, i) for i, j in up]
    last = lax.slice_in_dim(shard, length - width, length, axis=dim)
    first = lax.slice_in_dim(shard, 0, width, axis=dim)
    before = lax.ppermute(last, axis, up)
    after = lax.ppermute(first, axis, down)
    return before, after


def split_blur(mode, taps, shard, other, width):
    nz = shard.shape[0]
    before, after = halo_pair(shard, "gy", 1, width)
    rows_padded = jnp.concatenate([before, shard, after], axis=1)
    below, above = halo_pair(rows_padded, "gz", 0, width)
    inner = fused_blur(mode, [(0, nz - 2 * width, 0, width)], taps, rows_padded, other)
    low = edge_blur(mode, width, True, taps, below, rows_padded[: 2 * width], other[:width])
    high = edge_blur(mode, width, False, taps, above, rows_padded[nz - 2 * width :], other[nz - width :])
    volume = jnp.concatenate([low[0], inner[0], high[0]], axis=0)
    if mode == "update":
        return volume, jnp.maximum(jnp.maximum(inner[1], low[1]), high[1])
    return volume


def butterfly_max(value, axis):
    peers = lax.axis_size(axis)
    step = peers // 2
    while step >= 1:
        pairs = [(i, i ^ step) for i in range(peers)]
        value = jnp.maximum(value, lax.ppermute(value, axis, pairs))
        step //= 2
    return value


def per_device(observed, estimate, taps_z, taps_y, taps_x):
    radius = (taps_z.shape[0] - 1) // 2
    forward = jnp.concatenate([taps_z, taps_y, taps_x])
    backward = jnp.concatenate([taps_z[::-1], taps_y[::-1], taps_x[::-1]])
    ratio = split_blur("ratio", forward, estimate, observed, radius)
    updated, local_max = split_blur("update", backward, ratio, estimate, radius)
    projection = butterfly_max(local_max, "gz")
    return (updated, projection)


def solution(mesh):
    return jax.shard_map(
        per_device,
        mesh=mesh,
        in_specs=(P("gz", "gy", None), P("gz", "gy", None), P(), P(), P()),
        out_specs=(P("gz", "gy", None), P("gy", None)),
        check_vma=False,
    )
```

```python
import jax
import jax.numpy as jnp
from jax import lax
from jax.sharding import PartitionSpec as P
import functools
from jax.experimental import pallas as pl
from jax.experimental.pallas import tpu as pltpu


def blur_kernel(mode, segments, taps_ref, pad_ref, other_ref, out_ref, *rest):
    if mode == "update":
        max_ref, zbuf, ybuf = rest
    else:
        zbuf, ybuf = rest
    ntap = 9
    r = 4
    ny, nx = out_ref.shape[1], out_ref.shape[2]
    py = ny + 2 * r
    lanes = lax.broadcasted_iota(jnp.int32, (8, nx), 1)
    if mode == "update":
        max_ref[...] = jnp.full(max_ref.shape, -jnp.inf, max_ref.dtype)

    def plane(zo, zs, zt):
        for c in range(py // 8):
            rows = pl.ds(c * 8, 8)
            acc = taps_ref[0] * pad_ref[zs, rows, :]
            for k in range(1, ntap):
                acc = acc + taps_ref[k] * pad_ref[zs + k, rows, :]
            zbuf[rows, :] = acc
        for c in range(ny // 8):
            acc = taps_ref[ntap] * zbuf[pl.ds(c * 8, 8), :]
            for k in range(1, ntap):
                acc = acc + taps_ref[ntap + k] * zbuf[pl.ds(c * 8 + k, 8), :]
            ybuf[pl.ds(c * 8, 8), :] = acc
        for c in range(ny // 8):
            rows = pl.ds(c * 8, 8)
            v = ybuf[rows, :]
            acc = None
            for k in range(ntap):
                d = k - r
                if d == 0:
                    s = v
                else:
                    s = pltpu.roll(v, (-d) % nx, 1)
                    keep = (lanes >= -d) if d < 0 else (lanes < nx - d)
                    s = jnp.where(keep, s, 0.0)
                term = taps_ref[2 * ntap + k] * s
                acc = term if acc is None else acc + term
            if mode == "ratio":
                out_ref[zo, rows, :] = other_ref[zt, rows, :] / acc
            else:
                upd = other_ref[zt, rows, :] * acc
                out_ref[zo, rows, :] = upd
                max_ref[rows, :] = jnp.maximum(max_ref[rows, :], upd)

    for out_start, count, src_start, other_start in segments:
        def body(j, carry, out_start=out_start, src_start=src_start, other_start=other_start):
            plane(out_start + j, src_start + j, other_start + j)
            return carry

        lax.fori_loop(0, count, body, 0)


def fused_blur(mode, segments, taps, padded, other):
    nzo = sum(seg[1] for seg in segments)
    ny, nx = other.shape[1], other.shape[2]
    vmem = pltpu.VMEM
    outs = [jax.ShapeDtypeStruct((nzo, ny, nx), jnp.float32)]
    out_specs = [pl.BlockSpec(memory_space=vmem)]
    if mode == "update":
        outs.append(jax.ShapeDtypeStruct((ny, nx), jnp.float32))
        out_specs.append(pl.BlockSpec(memory_space=vmem))
    elems = nzo * ny * nx
    return pl.pallas_call(
        functools.partial(blur_kernel, mode, tuple(segments)),
        out_shape=tuple(outs),
        in_specs=[pl.BlockSpec(memory_space=pltpu.SMEM), pl.BlockSpec(memory_space=vmem), pl.BlockSpec(memory_space=vmem)],
        out_specs=tuple(out_specs),
        scratch_shapes=[pltpu.VMEM((ny + 8, nx), jnp.float32), pltpu.VMEM((ny, nx), jnp.float32)],
        compiler_params=pltpu.CompilerParams(vmem_limit_bytes=48 * 1024 * 1024),
        cost_estimate=pl.CostEstimate(flops=elems * 60, bytes_accessed=elems * 4 * 4, transcendentals=0),
    )(taps, padded, other)


def edge_kernel(mode, width, halo_first, taps_ref, halo_ref, own_ref, other_ref, out_ref, *rest):
    if mode == "update":
        max_ref, zbuf, ybuf = rest
        max_ref[...] = jnp.full(max_ref.shape, -jnp.inf, max_ref.dtype)
    else:
        (zbuf, ybuf), max_ref = rest, None
    ntap = 9
    r = 4
    ny, nx = out_ref.shape[1], out_ref.shape[2]
    py = ny + 2 * r
    lanes = lax.broadcasted_iota(jnp.int32, (8, nx), 1)
    for zo in range(width):

        def load(q, rows):
            if halo_first:
                return halo_ref[q, rows, :] if q < width else own_ref[q - width, rows, :]
            return own_ref[q, rows, :] if q < 2 * width else halo_ref[q - 2 * width, rows, :]

        for c in range(py // 8):
            rows = pl.ds(c * 8, 8)
            acc = taps_ref[0] * load(zo, rows)
            for k in range(1, ntap):
                acc = acc + taps_ref[k] * load(zo + k, rows)
            zbuf[rows, :] = acc
        for c in range(ny // 8):
            acc = taps_ref[ntap] * zbuf[pl.ds(c * 8, 8), :]
            for k in range(1, ntap):
                acc = acc + taps_ref[ntap + k] * zbuf[pl.ds(c * 8 + k, 8), :]
            ybuf[pl.ds(c * 8, 8), :] = acc
        for c in range(ny // 8):
            rows = pl.ds(c * 8, 8)
            v = ybuf[rows, :]
            acc = None
            for k in range(ntap):
                d = k - r
                if d == 0:
                    t = v
                else:
                    t = pltpu.roll(v, (-d) % nx, 1)
                    keep = (lanes >= -d) if d < 0 else (lanes < nx - d)
                    t = jnp.where(keep, t, 0.0)
                term = taps_ref[2 * ntap + k] * t
                acc = term if acc is None else acc + term
            if mode == "ratio":
                out_ref[zo, rows, :] = other_ref[zo, rows, :] / acc
            else:
                upd = other_ref[zo, rows, :] * acc
                out_ref[zo, rows, :] = upd
                max_ref[rows, :] = jnp.maximum(max_ref[rows, :], upd)


def edge_blur(mode, width, halo_first, taps, halo, own, other):
    nzo, ny, nx = other.shape
    vmem = pltpu.VMEM
    outs = [jax.ShapeDtypeStruct((nzo, ny, nx), jnp.float32)]
    out_specs = [pl.BlockSpec(memory_space=vmem)]
    if mode == "update":
        outs.append(jax.ShapeDtypeStruct((ny, nx), jnp.float32))
        out_specs.append(pl.BlockSpec(memory_space=vmem))
    elems = nzo * ny * nx
    return pl.pallas_call(
        functools.partial(edge_kernel, mode, width, halo_first),
        out_shape=tuple(outs),
        in_specs=[pl.BlockSpec(memory_space=pltpu.SMEM)] + [pl.BlockSpec(memory_space=vmem)] * 3,
        out_specs=tuple(out_specs),
        scratch_shapes=[pltpu.VMEM((ny + 8, nx), jnp.float32), pltpu.VMEM((ny, nx), jnp.float32)],
        compiler_params=pltpu.CompilerParams(vmem_limit_bytes=48 * 1024 * 1024),
        cost_estimate=pl.CostEstimate(flops=elems * 60, bytes_accessed=elems * 4 * 4, transcendentals=0),
    )(taps, halo, own, other)


def halo_pair(shard, axis, dim, width):
    peers, length = (lax.axis_size(axis), shard.shape[dim])
    up = [(i, (i + 1) % peers) for i in range(peers - 1)]
    down = [(j, i) for i, j in up]
    last = lax.slice_in_dim(shard, length - width, length, axis=dim)
    first = lax.slice_in_dim(shard, 0, width, axis=dim)
    before = lax.ppermute(last, axis, up)
    after = lax.ppermute(first, axis, down)
    return before, after


def split_blur(mode, taps, shard, other, width):
    nz = shard.shape[0]
    before, after = halo_pair(shard, "gy", 1, width)
    rows_padded = jnp.concatenate([before, shard, after], axis=1)
    below, above = halo_pair(rows_padded, "gz", 0, width)
    inner = fused_blur(mode, [(0, nz - 2 * width, 0, 0)], taps, rows_padded, other[width : nz - width])
    low = edge_blur(mode, width, True, taps, below, rows_padded[: 2 * width], other[:width])
    high = edge_blur(mode, width, False, taps, above, rows_padded[nz - 2 * width :], other[nz - width :])
    volume = jnp.concatenate([low[0], inner[0], high[0]], axis=0)
    if mode == "update":
        return volume, jnp.maximum(jnp.maximum(inner[1], low[1]), high[1])
    return volume


def butterfly_max(value, axis):
    peers = lax.axis_size(axis)
    step = peers // 2
    while step >= 1:
        pairs = [(i, i ^ step) for i in range(peers)]
        value = jnp.maximum(value, lax.ppermute(value, axis, pairs))
        step //= 2
    return value


def per_device(observed, estimate, taps_z, taps_y, taps_x):
    radius = (taps_z.shape[0] - 1) // 2
    forward = jnp.concatenate([taps_z, taps_y, taps_x])
    backward = jnp.concatenate([taps_z[::-1], taps_y[::-1], taps_x[::-1]])
    ratio = split_blur("ratio", forward, estimate, observed, radius)
    updated, local_max = split_blur("update", backward, ratio, estimate, radius)
    projection = butterfly_max(local_max, "gz")
    return (updated, projection)


def solution(mesh):
    return jax.shard_map(
        per_device,
        mesh=mesh,
        in_specs=(P("gz", "gy", None), P("gz", "gy", None), P(), P(), P()),
        out_specs=(P("gz", "gy", None), P("gy", None)),
        check_vma=False,
    )
```
